128 devices in a mesh: pair: 8 (over z, core), tile: 16 (over y, x).
Axes of the slice: x: 4, y: 4, z: 4, core: 2. Of those that a mesh axis runs over, the one named last changes fastest.
Arguments:
- phase: float32 [2000, 16, 1024], P('pair', 'tile'), may hold values from -12 to 12
- incidence: int32 [2000, 2], P('pair'), may hold values from 0 to 399, as said below
- pair_weight: float32 [2000], P('pair'), may hold values from 0.3 to 3
Outputs:
- solution_field: float32 [400, 16, 1024], P(None, 'tile', 'pair')
- residual: float32 [400, 16, 1024], P(None, 'tile', 'pair')
The draws below stay inside these ranges and needn't reach their ends.
Inputs may be any that keep to these rules, and one draw needn't show every extreme that they name: `incidence`: each row holds a reference date and a strictly later secondary date, at most 7 dates after the reference date; every pair of consecutive dates (t, t + 1) is some row.
All inputs are finite; a program needn't handle non-finite values.
Results may differ from the reference program's by a relative error of at most 0.00028.
Values sent between devices are 32-bit elements; how exact they have to be, the bound alone decides.
No kernel may reach another device: no remote copies, remote signals or barrier semaphores. Data moves between devices by JAX's collectives and lax.ppermute only.
A program may use at most 64 MiB of HBM per device.

```python
import math
import jax
import jax.numpy as jnp
from jax import lax

DATES = 400
PAIRS = 2000
COLS = 1024
ITERS = 3
ROWS = 16


def draw_incidence(key, part):
    first_key = jax.random.fold_in(key, 11)
    second_key = jax.random.fold_in(key, 23)
    order_key = jax.random.fold_in(key, 37)
    chain = jnp.arange(DATES - 1, dtype=jnp.int32)
    extra = PAIRS - (DATES - 1)
    starts = jax.random.randint(first_key, (extra,), 0, DATES - 1).astype(jnp.int32)
    spans = jax.random.randint(second_key, (extra,), 2, 8).astype(jnp.int32)
    ends = jnp.minimum(starts + spans, DATES - 1).astype(jnp.int32)
    earlier = jnp.concatenate([chain, starts])
    later = jnp.concatenate([chain + 1, ends])
    rows = jnp.stack([earlier, later], axis=1).astype(jnp.int32)
    order = jax.random.permutation(order_key, PAIRS)
    return rows[order].astype(jnp.int32)


def with_spikes(array, key, source, target, parts, factor):
    owner, partner = [(jnp.arange(array.shape[dim]) // (array.shape[dim] // parts)).reshape([-1 if axis == dim else 1 for axis in range(array.ndim)]) for dim in (source, target)]
    chosen = jax.random.permutation(key, parts)[partner]
    strong = (owner == chosen) | (owner == (partner + parts // 2) % parts)
    return jnp.where(strong, factor * array, array)


def steps_of(own_key, extent, cuts, least, largest):
    gain, own = 1.0, jax.random.fold_in(own_key, 6)
    for dim, blocks in cuts:
        steps = jnp.exp(jax.random.uniform(jax.random.fold_in(own, dim), (blocks,), jnp.float32, least / len(cuts), largest / len(cuts)))
        gain = gain * jnp.repeat(steps, extent[dim] // blocks).reshape([-1 if axis == dim else 1 for axis in range(len(extent))])
    return gain


def bell_draw_with(rng, shape, width, reach, shards, heavy, held_as=jnp.bfloat16):
    values = width * jax.random.normal(rng, shape, jnp.float32)
    if shards:
        values = values * steps_of(rng, shape, shards, -0.22, 0.18)
    return jnp.clip(with_spikes(values, jax.random.fold_in(rng, 3), *heavy), -reach, reach).astype(held_as)


def setup_inputs(seed: int = 0) -> dict:
    seeds = jax.random.split(jax.random.key(seed), 4)
    phase = bell_draw_with(seeds[0], (PAIRS, ROWS, COLS), 3.0, 12.0, ((0, 8), (1, 16)), (0, 2, 8, 2.0), jnp.float32)
    incidence = draw_incidence(jax.random.fold_in(seeds[3], 71), 0)
    pair_weight = jnp.clip(jnp.exp(math.log(3.0) - 2.3025851 * jax.random.uniform(seeds[2], (PAIRS,), jnp.float32) ** steps_of(seeds[2], (PAIRS,), ((0, 8),), -0.2, 0.2)), 0.3, 3.0)
    return {"phase": phase, "incidence": incidence, "pair_weight": pair_weight}


temporal_weight = 2.0
spatial_weight = 0.5
ridge_weight = 0.05


def design(incidence):
    dates = jnp.arange(DATES, dtype=jnp.int32)
    later = (dates[None, :] == incidence[:, 1:2]).astype(jnp.float32)
    earlier = (dates[None, :] == incidence[:, 0:1]).astype(jnp.float32)
    return later - earlier


def regularize(field):
    second = field[:-2] - 2.0 * field[1:-1] + field[2:]
    temporal = jnp.pad(second, ((2, 0), (0, 0), (0, 0))) - 2.0 * jnp.pad(second, ((1, 1), (0, 0), (0, 0))) + jnp.pad(second, ((0, 2), (0, 0), (0, 0)))
    padded = jnp.pad(field, ((0, 0), (1, 1), (1, 1)))
    spatial = 4.0 * field - padded[:, 2:, 1:-1] - padded[:, :-2, 1:-1] - padded[:, 1:-1, 2:] - padded[:, 1:-1, :-2]
    return temporal_weight * temporal + spatial_weight * spatial + ridge_weight * field


def operate(field, network, pair_weight):
    forward = jnp.einsum("kt,trc->krc", network, field, precision=lax.Precision.HIGHEST)
    backward = jnp.einsum("kt,krc->trc", network, pair_weight[:, None, None] * forward, precision=lax.Precision.HIGHEST)
    return backward + regularize(field)


def reference(phase, incidence, pair_weight):
    network = design(incidence)
    right_side = jnp.einsum("kt,krc->trc", network, pair_weight[:, None, None] * phase, precision=lax.Precision.HIGHEST)
    solution_field = jnp.zeros_like(right_side)
    residual = right_side
    direction = right_side
    norm_now = jnp.sum(residual * residual)
    for iteration in range(ITERS):
        image = operate(direction, network, pair_weight)
        alpha = norm_now / jnp.sum(direction * image)
        solution_field = solution_field + alpha * direction
        residual = residual - alpha * image
        norm_next = jnp.sum(residual * residual)
        direction = residual + (norm_next / norm_now) * direction
        norm_now = norm_next
    return solution_field, residual
```

```python
import numpy as np
import jax
import jax.numpy as jnp
from jax import lax
from jax.sharding import PartitionSpec as P

DATES = 400
ITERS = 3
SPAN = 8

temporal_weight = 2.0
spatial_weight = 0.5
ridge_weight = 0.05

HIGHEST = lax.Precision.HIGHEST


def temporal_matrix():
    second = np.zeros((DATES - 2, DATES), np.float64)
    rows = np.arange(DATES - 2)
    second[rows, rows] = 1.0
    second[rows, rows + 1] = -2.0
    second[rows, rows + 2] = 1.0
    return (second.T @ second).astype(np.float32)


def from_prev(cells, axis):
    count = lax.axis_size(axis)
    return lax.ppermute(cells, axis, [(i, i + 1) for i in range(count - 1)])


def from_next(cells, axis):
    count = lax.axis_size(axis)
    return lax.ppermute(cells, axis, [(i + 1, i) for i in range(count - 1)])


def exchange(cells):
    return (
        from_prev(cells, "tile"),
        from_next(cells, "tile"),
        from_prev(cells[:, -1:], "pair"),
        from_next(cells[:, :1], "pair"),
    )


def neighbours(cells, halo):
    above, below, left, right = halo
    west = jnp.concatenate([left, cells[:, :-1]], axis=1)
    east = jnp.concatenate([cells[:, 1:], right], axis=1)
    return above + below + west + east


def apply_operator(matrix, cells, halo):
    return jnp.dot(matrix, cells, precision=HIGHEST) - spatial_weight * neighbours(cells, halo)


def total(parts):
    count = lax.axis_size("pair") * lax.axis_size("tile")
    sent = jnp.broadcast_to(parts[None, :], (count, parts.shape[0]))
    got = lax.all_to_all(sent, ("pair", "tile"), 0, 0, tiled=True)
    return jnp.sum(got, axis=0)


def normal_matrix(weights):
    dates = jnp.arange(DATES, dtype=jnp.int32)
    offset = dates[None, :] - dates[:, None]
    upper = jnp.zeros((DATES, DATES), jnp.float32)
    for d in range(1, SPAN):
        upper = upper + jnp.where(offset == d, -weights[:, d : d + 1], 0.0)
    coupling = upper + upper.T
    degree = -jnp.sum(coupling, axis=1)
    diagonal = degree + (4.0 * spatial_weight + ridge_weight)
    return coupling + jnp.where(offset == 0, diagonal[:, None], 0.0) + temporal_weight * temporal_matrix()


def body(phase, incidence, pair_weight):
    groups = lax.axis_size("pair")
    cols = phase.shape[2] // groups
    dates = jnp.arange(DATES, dtype=jnp.int32)
    earlier = incidence[:, 0:1]
    later = incidence[:, 1:2]
    network = (dates[None, :] == later).astype(jnp.float32) - (dates[None, :] == earlier).astype(jnp.float32)
    weighted = (pair_weight[:, None] * phase[:, 0, :]).reshape(-1, groups, cols)
    part = jnp.einsum("kt,kjc->jtc", network, weighted, precision=HIGHEST)
    span_hot = (jnp.arange(SPAN, dtype=jnp.int32)[None, :] == (later - earlier)).astype(jnp.float32)
    start_hot = (dates[None, :] == earlier).astype(jnp.float32)
    span_weights = jnp.einsum("kt,kd->td", start_hot, span_hot * pair_weight[:, None], precision=HIGHEST)
    stacked = jnp.concatenate([part, jnp.broadcast_to(span_weights, (groups, DATES, SPAN))], axis=2)
    reduced = lax.psum_scatter(stacked, "pair", scatter_dimension=0, tiled=True)[0]
    residual = reduced[:, :cols]
    matrix = normal_matrix(reduced[:, cols:])

    residual_halo = exchange(residual)
    solution_field = jnp.zeros_like(residual)
    for iteration in range(ITERS):
        image_of_residual = apply_operator(matrix, residual, residual_halo)
        if iteration == 0:
            parts = jnp.stack([jnp.sum(residual * residual), jnp.sum(residual * image_of_residual)])
        else:
            parts = jnp.stack(
                [
                    jnp.sum(residual * residual),
                    jnp.sum(residual * image_of_residual),
                    jnp.sum(residual * image),
                    jnp.sum(direction * image_of_residual),
                    jnp.sum(direction * image),
                ]
            )
        if iteration < ITERS - 1:
            image_halo = exchange(image_of_residual)
        sums = total(parts)
        norm_now = sums[0]
        if iteration == 0:
            alpha = norm_now / sums[1]
            direction = residual
            image = image_of_residual
            if iteration < ITERS - 1:
                halo_image = image_halo
        else:
            beta = norm_now / norm_prev
            curvature = sums[1] + beta * (sums[2] + sums[3]) + beta * beta * sums[4]
            alpha = norm_now / curvature
            direction = residual + beta * direction
            image = image_of_residual + beta * image
            if iteration < ITERS - 1:
                halo_image = tuple(a + beta * b for a, b in zip(image_halo, halo_image))
        solution_field = solution_field + alpha * direction
        residual = residual - alpha * image
        if iteration < ITERS - 1:
            residual_halo = tuple(a - alpha * b for a, b in zip(residual_halo, halo_image))
        norm_prev = norm_now
    return (solution_field[:, None, :], residual[:, None, :])


def solution(mesh):
    return jax.shard_map(
        body,
        mesh=mesh,
        in_specs=(P("pair", "tile", None), P("pair", None), P("pair")),
        out_specs=(P(None, "tile", "pair"), P(None, "tile", "pair")),
        check_vma=False,
    )
```

```python
import numpy as np
import jax
import jax.numpy as jnp
from jax import lax
from jax.sharding import PartitionSpec as P

DATES = 400
ITERS = 3
SPAN = 8

temporal_weight = 2.0
spatial_weight = 0.5
ridge_weight = 0.05

HIGHEST = lax.Precision.HIGHEST


def temporal_matrix():
    second = np.zeros((DATES - 2, DATES), np.float64)
    rows = np.arange(DATES - 2)
    second[rows, rows] = 1.0
    second[rows, rows + 1] = -2.0
    second[rows, rows + 2] = 1.0
    return (second.T @ second).astype(np.float32)


def from_prev(cells, axis):
    count = lax.axis_size(axis)
    return lax.ppermute(cells, axis, [(i, i + 1) for i in range(count - 1)])


def from_next(cells, axis):
    count = lax.axis_size(axis)
    return lax.ppermute(cells, axis, [(i + 1, i) for i in range(count - 1)])


def exchange(cells):
    return (
        from_prev(cells, "tile"),
        from_next(cells, "tile"),
        from_prev(cells[:, -1:], "pair"),
        from_next(cells[:, :1], "pair"),
    )


def neighbours(cells, halo):
    above, below, left, right = halo
    west = jnp.concatenate([left, cells[:, :-1]], axis=1)
    east = jnp.concatenate([cells[:, 1:], right], axis=1)
    return above + below + west + east


def apply_operator(matrix, cells, halo):
    return jnp.dot(matrix, cells, precision=HIGHEST) - spatial_weight * neighbours(cells, halo)


def total(parts):
    count = lax.axis_size("pair") * lax.axis_size("tile")
    sent = jnp.broadcast_to(parts[None, :], (count, parts.shape[0]))
    got = lax.all_to_all(sent, ("pair", "tile"), 0, 0, tiled=True)
    return jnp.sum(got, axis=0)


def normal_matrix(weights):
    dates = jnp.arange(DATES, dtype=jnp.int32)
    offset = dates[None, :] - dates[:, None]
    upper = jnp.zeros((DATES, DATES), jnp.float32)
    for d in range(1, SPAN):
        upper = upper + jnp.where(offset == d, -weights[:, d : d + 1], 0.0)
    coupling = upper + upper.T
    degree = -jnp.sum(coupling, axis=1)
    diagonal = degree + (4.0 * spatial_weight + ridge_weight)
    return coupling + jnp.where(offset == 0, diagonal[:, None], 0.0) + temporal_weight * temporal_matrix()


def body(phase, incidence, pair_weight):
    groups = lax.axis_size("pair")
    cols = phase.shape[2] // groups
    padded = jnp.pad(phase[:, 0, :], ((0, 0), (1, 1)))
    windows = jnp.stack([padded[:, j * cols : j * cols + cols + 2] for j in range(groups)])
    meta = jnp.stack(
        [incidence[:, 0].astype(jnp.float32), incidence[:, 1].astype(jnp.float32), pair_weight], axis=1
    )
    meta = jnp.pad(meta, ((0, 0), (0, 3)))
    chunks = jnp.concatenate([windows, jnp.broadcast_to(meta, (groups,) + meta.shape)], axis=2)
    got = lax.all_to_all(chunks, "pair", 0, 0, tiled=True).reshape(-1, chunks.shape[2])
    values = got[:, : cols + 2]
    earlier = got[:, cols + 2 : cols + 3]
    later = got[:, cols + 3 : cols + 4]
    weight = got[:, cols + 4 : cols + 5]
    dates = jnp.arange(DATES, dtype=jnp.float32)
    network = (dates[None, :] == later).astype(jnp.float32) - (dates[None, :] == earlier).astype(jnp.float32)
    right_wide = jnp.einsum("kt,kc->tc", network, weight * values, precision=HIGHEST)
    span_hot = (jnp.arange(SPAN, dtype=jnp.float32)[None, :] == (later - earlier)).astype(jnp.float32)
    start_hot = (dates[None, :] == earlier).astype(jnp.float32)
    span_weights = jnp.einsum("kt,kd->td", start_hot, span_hot * weight, precision=HIGHEST)
    matrix = normal_matrix(span_weights)
    residual = right_wide[:, 1:-1]
    residual_halo = (
        from_prev(residual, "tile"),
        from_next(residual, "tile"),
        right_wide[:, :1],
        right_wide[:, -1:],
    )
    solution_field = jnp.zeros_like(residual)
    for iteration in range(ITERS):
        image_of_residual = apply_operator(matrix, residual, residual_halo)
        if iteration == 0:
            parts = jnp.stack([jnp.sum(residual * residual), jnp.sum(residual * image_of_residual)])
        else:
            parts = jnp.stack(
                [
                    jnp.sum(residual * residual),
                    jnp.sum(residual * image_of_residual),
                    jnp.sum(residual * image),
                    jnp.sum(direction * image_of_residual),
                    jnp.sum(direction * image),
                ]
            )
        if iteration < ITERS - 1:
            image_halo = exchange(image_of_residual)
        sums = total(parts)
        norm_now = sums[0]
        if iteration == 0:
            alpha = norm_now / sums[1]
            direction = residual
            image = image_of_residual
            if iteration < ITERS - 1:
                halo_image = image_halo
        else:
            beta = norm_now / norm_prev
            curvature = sums[1] + beta * (sums[2] + sums[3]) + beta * beta * sums[4]
            alpha = norm_now / curvature
            direction = residual + beta * direction
            image = image_of_residual + beta * image
            if iteration < ITERS - 1:
                halo_image = tuple(a + beta * b for a, b in zip(image_halo, halo_image))
        solution_field = solution_field + alpha * direction
        residual = residual - alpha * image
        if iteration < ITERS - 1:
            residual_halo = tuple(a - alpha * b for a, b in zip(residual_halo, halo_image))
        norm_prev = norm_now
    return (solution_field[:, None, :], residual[:, None, :])


def solution(mesh):
    return jax.shard_map(
        body,
        mesh=mesh,
        in_specs=(P("pair", "tile", None), P("pair", None), P("pair")),
        out_specs=(P(None, "tile", "pair"), P(None, "tile", "pair")),
        check_vma=False,
    )
```

```python
import numpy as np
import jax
import jax.numpy as jnp
from jax import lax
from jax.sharding import PartitionSpec as P

DATES = 400
ITERS = 3
SPAN = 8

temporal_weight = 2.0
spatial_weight = 0.5
ridge_weight = 0.05

HIGHEST = lax.Precision.HIGHEST


def temporal_matrix():
    second = np.zeros((DATES - 2, DATES), np.float64)
    rows = np.arange(DATES - 2)
    second[rows, rows] = 1.0
    second[rows, rows + 1] = -2.0
    second[rows, rows + 2] = 1.0
    return (second.T @ second).astype(np.float32)


def from_prev(cells, axis):
    count = lax.axis_size(axis)
    return lax.ppermute(cells, axis, [(i, i + 1) for i in range(count - 1)])


def from_next(cells, axis):
    count = lax.axis_size(axis)
    return lax.ppermute(cells, axis, [(i + 1, i) for i in range(count - 1)])


def exchange(cells):
    return (
        from_prev(cells, "tile"),
        from_next(cells, "tile"),
        from_prev(cells[:, -1:], "pair"),
        from_next(cells[:, :1], "pair"),
    )


def neighbours(cells, halo):
    above, below, left, right = halo
    west = jnp.concatenate([left, cells[:, :-1]], axis=1)
    east = jnp.concatenate([cells[:, 1:], right], axis=1)
    return above + below + west + east


def apply_operator(matrix, cells, halo):
    return jnp.dot(matrix, cells, precision=HIGHEST) - spatial_weight * neighbours(cells, halo)


def total(parts):
    count = lax.axis_size("pair") * lax.axis_size("tile")
    sent = jnp.broadcast_to(parts[None, :], (count, parts.shape[0]))
    got = lax.all_to_all(sent, ("pair", "tile"), 0, 0, tiled=True)
    return jnp.sum(got, axis=0)


def normal_matrix(weights):
    dates = jnp.arange(DATES, dtype=jnp.int32)
    offset = dates[None, :] - dates[:, None]
    upper = jnp.zeros((DATES, DATES), jnp.float32)
    for d in range(1, SPAN):
        upper = upper + jnp.where(offset == d, -weights[:, d : d + 1], 0.0)
    coupling = upper + upper.T
    degree = -jnp.sum(coupling, axis=1)
    diagonal = degree + (4.0 * spatial_weight + ridge_weight)
    return coupling + jnp.where(offset == 0, diagonal[:, None], 0.0) + temporal_weight * temporal_matrix()


def body(phase, incidence, pair_weight):
    groups = lax.axis_size("pair")
    cols = phase.shape[2] // groups
    padded = jnp.pad(phase[:, 0, :], ((0, 0), (1, 1)))
    windows = jnp.stack([padded[:, j * cols : j * cols + cols + 2] for j in range(groups)])
    meta = jnp.stack(
        [incidence[:, 0].astype(jnp.float32), incidence[:, 1].astype(jnp.float32), pair_weight], axis=1
    )
    meta = jnp.pad(meta, ((0, 0), (0, 3)))
    chunks = jnp.concatenate([windows, jnp.broadcast_to(meta, (groups,) + meta.shape)], axis=2)
    got = lax.all_to_all(chunks, "pair", 0, 0, tiled=True).reshape(-1, chunks.shape[2])
    values = got[:, : cols + 2]
    earlier = got[:, cols + 2 : cols + 3]
    later = got[:, cols + 3 : cols + 4]
    weight = got[:, cols + 4 : cols + 5]
    dates = jnp.arange(DATES, dtype=jnp.float32)
    network = (dates[None, :] == later).astype(jnp.float32) - (dates[None, :] == earlier).astype(jnp.float32)
    right_wide = jnp.einsum("kt,kc->tc", network, weight * values, precision=HIGHEST)
    span_hot = (jnp.arange(SPAN, dtype=jnp.float32)[None, :] == (later - earlier)).astype(jnp.float32)
    start_hot = (dates[None, :] == earlier).astype(jnp.float32)
    span_weights = jnp.einsum("kt,kd->td", start_hot, span_hot * weight, precision=HIGHEST)
    matrix = normal_matrix(span_weights)
    residual = right_wide[:, 1:-1]
    residual_halo = (
        from_prev(residual, "tile"),
        from_next(residual, "tile"),
        right_wide[:, :1],
        right_wide[:, -1:],
    )
    solution_field = jnp.zeros_like(residual)
    for iteration in range(ITERS):
        image_of_residual = apply_operator(matrix, residual, residual_halo)
        if iteration == 0:
            products = [residual * residual, residual * image_of_residual]
        else:
            products = [
                residual * residual,
                residual * image_of_residual,
                residual * image,
                direction * image_of_residual,
                direction * image,
            ]
        parts = jnp.sum(jnp.stack(products), axis=(1, 2))
        if iteration < ITERS - 1:
            image_halo = exchange(image_of_residual)
        sums = total(parts)[:, None]
        norm_now = sums[0:1]
        if iteration == 0:
            alpha = norm_now / sums[1:2]
            direction = residual
            image = image_of_residual
            if iteration < ITERS - 1:
                halo_image = image_halo
        else:
            beta = norm_now / norm_prev
            curvature = sums[1:2] + beta * (sums[2:3] + sums[3:4]) + beta * beta * sums[4:5]
            alpha = norm_now / curvature
            direction = residual + beta * direction
            image = image_of_residual + beta * image
            if iteration < ITERS - 1:
                halo_image = tuple(a + beta * b for a, b in zip(image_halo, halo_image))
        solution_field = solution_field + alpha * direction
        residual = residual - alpha * image
        if iteration < ITERS - 1:
            residual_halo = tuple(a - alpha * b for a, b in zip(residual_halo, halo_image))
        norm_prev = norm_now
    return (solution_field[:, None, :], residual[:, None, :])


def solution(mesh):
    return jax.shard_map(
        body,
        mesh=mesh,
        in_specs=(P("pair", "tile", None), P("pair", None), P("pair")),
        out_specs=(P(None, "tile", "pair"), P(None, "tile", "pair")),
        check_vma=False,
    )
```

```python
import numpy as np
import jax
import jax.numpy as jnp
from jax import lax
from jax.sharding import PartitionSpec as P
from jax.experimental import pallas as pl
from jax.experimental.pallas import tpu as pltpu

DATES = 400
ITERS = 3
SPAN = 8

temporal_weight = 2.0
spatial_weight = 0.5
ridge_weight = 0.05

HIGHEST = lax.Precision.HIGHEST


def temporal_matrix():
    second = np.zeros((DATES - 2, DATES), np.float64)
    rows = np.arange(DATES - 2)
    second[rows, rows] = 1.0
    second[rows, rows + 1] = -2.0
    second[rows, rows + 2] = 1.0
    return (second.T @ second).astype(np.float32)


def from_prev(cells, axis):
    count = lax.axis_size(axis)
    return lax.ppermute(cells, axis, [(i, i + 1) for i in range(count - 1)])


def from_next(cells, axis):
    count = lax.axis_size(axis)
    return lax.ppermute(cells, axis, [(i + 1, i) for i in range(count - 1)])


def exchange(cells):
    return (
        from_prev(cells, "tile"),
        from_next(cells, "tile"),
        from_prev(cells[:, -1:], "pair"),
        from_next(cells[:, :1], "pair"),
    )


def neighbours(cells, halo):
    above, below, left, right = halo
    west = jnp.concatenate([left, cells[:, :-1]], axis=1)
    east = jnp.concatenate([cells[:, 1:], right], axis=1)
    return above + below + west + east


def apply_operator(matrix, cells, halo):
    return jnp.dot(matrix, cells, precision=HIGHEST) - spatial_weight * neighbours(cells, halo)


def total(parts):
    count = lax.axis_size("pair") * lax.axis_size("tile")
    sent = jnp.broadcast_to(parts[None, :], (count, parts.shape[0]))
    got = lax.all_to_all(sent, ("pair", "tile"), 0, 0, tiled=True)
    return jnp.sum(got, axis=0)


def normal_matrix(weights):
    dates = jnp.arange(DATES, dtype=jnp.int32)
    offset = dates[None, :] - dates[:, None]
    upper = jnp.zeros((DATES, DATES), jnp.float32)
    for d in range(1, SPAN):
        upper = upper + jnp.where(offset == d, -weights[:, d : d + 1], 0.0)
    coupling = upper + upper.T
    degree = -jnp.sum(coupling, axis=1)
    diagonal = degree + (4.0 * spatial_weight + ridge_weight)
    return coupling + jnp.where(offset == 0, diagonal[:, None], 0.0) + temporal_weight * temporal_matrix()


def lane_value(vector, j):
    lanes = lax.broadcasted_iota(jnp.int32, vector.shape, 1)
    return jnp.sum(jnp.where(lanes == j, vector, 0.0), axis=1, keepdims=True)


def shifted(cells, left, right):
    width = cells.shape[1]
    lanes = lax.broadcasted_iota(jnp.int32, cells.shape, 1)
    probe = pltpu.roll(lanes, 1, 1)
    forward = probe == jnp.where(lanes == 0, width - 1, lanes - 1)
    one = pltpu.roll(cells, 1, 1)
    back = pltpu.roll(cells, width - 1, 1)
    west = jnp.where(lanes == 0, left, jnp.where(forward, one, back))
    east = jnp.where(lanes == width - 1, right, jnp.where(forward, back, one))
    return west, east


def operate(matrix, cells, above, below, left, right):
    west, east = shifted(cells, left, right)
    return jnp.dot(matrix, cells, precision=HIGHEST, preferred_element_type=jnp.float32) - spatial_weight * (
        above + below + west + east
    )


def send_buffer(send_ref, values):
    lanes = lax.broadcasted_iota(jnp.int32, (1, send_ref.shape[1]), 1)
    row = jnp.zeros((1, send_ref.shape[1]), jnp.float32)
    for j, value in enumerate(values):
        row = row + jnp.where(lanes == j, jnp.sum(value, keepdims=True), 0.0)
    send_ref[...] = jnp.broadcast_to(row, send_ref.shape)


def first_kernel(k_ref, r_ref, ru_ref, rd_ref, rl_ref, rr_ref, w_ref, send_ref):
    r = r_ref[...]
    w = operate(k_ref[...], r, ru_ref[...], rd_ref[...], rl_ref[...], rr_ref[...])
    w_ref[...] = w
    send_buffer(send_ref, [r * r, r * w])


def second_kernel(got_ref, k_ref, r_ref, ru_ref, rd_ref, rl_ref, rr_ref, w_ref, wu_ref, wd_ref, wl_ref, wr_ref,
                  r_out, x_out, w_out, send_ref, scal_ref):
    sums = jnp.sum(got_ref[...], axis=0, keepdims=True)
    norm = lane_value(sums, 0)
    alpha = norm / lane_value(sums, 1)
    p = r_ref[...]
    q = w_ref[...]
    x_out[...] = alpha * p
    r = p - alpha * q
    r_out[...] = r
    halo = [h[...] - alpha * g[...] for h, g in zip((ru_ref, rd_ref, rl_ref, rr_ref), (wu_ref, wd_ref, wl_ref, wr_ref))]
    w = operate(k_ref[...], r, *halo)
    w_out[...] = w
    send_buffer(send_ref, [r * r, r * w, r * q, p * w, p * q])
    lanes = lax.broadcasted_iota(jnp.int32, scal_ref.shape, 1)
    scal_ref[...] = jnp.where(lanes == 0, norm, jnp.where(lanes == 1, alpha, 0.0))


def step_scalars(got_ref, scal_ref):
    sums = jnp.sum(got_ref[...], axis=0, keepdims=True)
    previous = scal_ref[...]
    norm = lane_value(sums, 0)
    beta = norm / lane_value(previous, 0)
    curvature = lane_value(sums, 1) + beta * (lane_value(sums, 2) + lane_value(sums, 3)) + beta * beta * lane_value(sums, 4)
    return norm, beta, norm / curvature


def third_kernel(got_ref, scal_ref, k_ref, r_ref, p_ref, q_ref, x_ref, w_ref,
                 ru_ref, rd_ref, rl_ref, rr_ref, qu_ref, qd_ref, ql_ref, qr_ref, wu_ref, wd_ref, wl_ref, wr_ref,
                 r_out, p_out, q_out, x_out, w_out, send_ref, scal_out):
    norm, beta, alpha = step_scalars(got_ref, scal_ref)
    alpha_first = lane_value(scal_ref[...], 1)
    p = r_ref[...] + beta * p_ref[...]
    q = w_ref[...] + beta * q_ref[...]
    p_out[...] = p
    q_out[...] = q
    x_out[...] = x_ref[...] + alpha * p
    r = r_ref[...] - alpha * q
    r_out[...] = r
    halo = []
    for h, k, g in zip((ru_ref, rd_ref, rl_ref, rr_ref), (qu_ref, qd_ref, ql_ref, qr_ref), (wu_ref, wd_ref, wl_ref, wr_ref)):
        halo.append((h[...] - alpha_first * k[...]) - alpha * (g[...] + beta * k[...]))
    w = operate(k_ref[...], r, *halo)
    w_out[...] = w
    send_buffer(send_ref, [r * r, r * w, r * q, p * w, p * q])
    lanes = lax.broadcasted_iota(jnp.int32, scal_out.shape, 1)
    scal_out[...] = jnp.where(lanes == 0, norm, jnp.where(lanes == 1, alpha, 0.0))


def last_kernel(got_ref, scal_ref, r_ref, p_ref, q_ref, x_ref, w_ref, x_out, r_out):
    norm, beta, alpha = step_scalars(got_ref, scal_ref)
    p = r_ref[...] + beta * p_ref[...]
    q = w_ref[...] + beta * q_ref[...]
    x_out[...] = x_ref[...] + alpha * p
    r_out[...] = r_ref[...] - alpha * q


def call(kernel, shapes, *args):
    return pl.pallas_call(kernel, out_shape=[jax.ShapeDtypeStruct(s, jnp.float32) for s in shapes])(*args)


def reduce_all(send):
    return lax.all_to_all(send, ("pair", "tile"), 0, 0, tiled=True)


def exchange_rows_cols(cells):
    return (
        from_prev(cells, "tile"),
        from_next(cells, "tile"),
        from_prev(cells[:, -1:], "pair"),
        from_next(cells[:, :1], "pair"),
    )


def body(phase, incidence, pair_weight):
    groups = lax.axis_size("pair")
    cols = phase.shape[2] // groups
    padded = jnp.pad(phase[:, 0, :], ((0, 0), (1, 1)))
    windows = jnp.stack([padded[:, j * cols : j * cols + cols + 2] for j in range(groups)])
    meta = jnp.stack(
        [incidence[:, 0].astype(jnp.float32), incidence[:, 1].astype(jnp.float32), pair_weight], axis=1
    )
    meta = jnp.pad(meta, ((0, 0), (0, 3)))
    chunks = jnp.concatenate([windows, jnp.broadcast_to(meta, (groups,) + meta.shape)], axis=2)
    got = lax.all_to_all(chunks, "pair", 0, 0, tiled=True).reshape(-1, chunks.shape[2])
    values = got[:, : cols + 2]
    earlier = got[:, cols + 2 : cols + 3]
    later = got[:, cols + 3 : cols + 4]
    weight = got[:, cols + 4 : cols + 5]
    dates = jnp.arange(DATES, dtype=jnp.float32)
    network = (dates[None, :] == later).astype(jnp.float32) - (dates[None, :] == earlier).astype(jnp.float32)
    right_wide = jnp.einsum("kt,kc->tc", network, weight * values, precision=HIGHEST)
    span_hot = (jnp.arange(SPAN, dtype=jnp.float32)[None, :] == (later - earlier)).astype(jnp.float32)
    start_hot = (dates[None, :] == earlier).astype(jnp.float32)
    span_weights = jnp.einsum("kt,kd->td", start_hot, span_hot * weight, precision=HIGHEST)
    matrix = normal_matrix(span_weights)
    residual = right_wide[:, 1:-1]
    residual_halo = (
        from_prev(residual, "tile"),
        from_next(residual, "tile"),
        right_wide[:, :1],
        right_wide[:, -1:],
    )
    count = lax.axis_size("pair") * lax.axis_size("tile")
    field = residual.shape
    lanes = 128
    send_shape = (count, lanes)
    w0, send = call(first_kernel, [field, send_shape], matrix, residual, *residual_halo)
    w0_halo = exchange_rows_cols(w0)
    got = reduce_all(send)
    r1, x1, w1, send, scal = call(
        second_kernel, [field, field, field, send_shape, (1, lanes)], got, matrix, residual, *residual_halo, w0, *w0_halo
    )
    w1_halo = exchange_rows_cols(w1)
    got = reduce_all(send)
    r2, p1, q1, x2, w2, send, scal = call(
        third_kernel,
        [field, field, field, field, field, send_shape, (1, lanes)],
        got, scal, matrix, r1, residual, w0, x1, w1, *residual_halo, *w0_halo, *w1_halo,
    )
    got = reduce_all(send)
    solution_field, residual = call(last_kernel, [field, field], got, scal, r2, p1, q1, x2, w2)
    return (solution_field[:, None, :], residual[:, None, :])


def solution(mesh):
    return jax.shard_map(
        body,
        mesh=mesh,
        in_specs=(P("pair", "tile", None), P("pair", None), P("pair")),
        out_specs=(P(None, "tile", "pair"), P(None, "tile", "pair")),
        check_vma=False,
    )
```

```python
import numpy as np
import jax
import jax.numpy as jnp
from jax import lax
from jax.sharding import PartitionSpec as P
from jax.experimental import pallas as pl
from jax.experimental.pallas import tpu as pltpu

DATES = 400
ITERS = 3
SPAN = 8

temporal_weight = 2.0
spatial_weight = 0.5
ridge_weight = 0.05

HIGHEST = lax.Precision.HIGHEST


def temporal_matrix():
    second = np.zeros((DATES - 2, DATES), np.float64)
    rows = np.arange(DATES - 2)
    second[rows, rows] = 1.0
    second[rows, rows + 1] = -2.0
    second[rows, rows + 2] = 1.0
    return (second.T @ second).astype(np.float32)


def from_prev(cells, axis):
    count = lax.axis_size(axis)
    return lax.ppermute(cells, axis, [(i, i + 1) for i in range(count - 1)])


def from_next(cells, axis):
    count = lax.axis_size(axis)
    return lax.ppermute(cells, axis, [(i + 1, i) for i in range(count - 1)])


def exchange(cells):
    return (
        from_prev(cells, "tile"),
        from_next(cells, "tile"),
        from_prev(cells[:, -1:], "pair"),
        from_next(cells[:, :1], "pair"),
    )


def neighbours(cells, halo):
    above, below, left, right = halo
    west = jnp.concatenate([left, cells[:, :-1]], axis=1)
    east = jnp.concatenate([cells[:, 1:], right], axis=1)
    return above + below + west + east


def apply_operator(matrix, cells, halo):
    return jnp.dot(matrix, cells, precision=HIGHEST) - spatial_weight * neighbours(cells, halo)


def total(parts):
    count = lax.axis_size("pair") * lax.axis_size("tile")
    sent = jnp.broadcast_to(parts[None, :], (count, parts.shape[0]))
    got = lax.all_to_all(sent, ("pair", "tile"), 0, 0, tiled=True)
    return jnp.sum(got, axis=0)


def normal_matrix(weights):
    dates = jnp.arange(DATES, dtype=jnp.int32)
    offset = dates[None, :] - dates[:, None]
    upper = jnp.zeros((DATES, DATES), jnp.float32)
    for d in range(1, SPAN):
        upper = upper + jnp.where(offset == d, -weights[:, d : d + 1], 0.0)
    coupling = upper + upper.T
    degree = -jnp.sum(coupling, axis=1)
    diagonal = degree + (4.0 * spatial_weight + ridge_weight)
    return coupling + jnp.where(offset == 0, diagonal[:, None], 0.0) + temporal_weight * temporal_matrix()


def lane_value(vector, j):
    lanes = lax.broadcasted_iota(jnp.int32, vector.shape, 1)
    return jnp.sum(jnp.where(lanes == j, vector, 0.0), axis=1, keepdims=True)


def shifted(cells, left, right):
    width = cells.shape[1]
    lanes = lax.broadcasted_iota(jnp.int32, cells.shape, 1)
    probe = pltpu.roll(lanes, 1, 1)
    forward = probe == jnp.where(lanes == 0, width - 1, lanes - 1)
    one = pltpu.roll(cells, 1, 1)
    back = pltpu.roll(cells, width - 1, 1)
    west = jnp.where(lanes == 0, left, jnp.where(forward, one, back))
    east = jnp.where(lanes == width - 1, right, jnp.where(forward, back, one))
    return west, east


def operate(matrix, cells, above, below, left, right):
    west, east = shifted(cells, left, right)
    return jnp.dot(matrix, cells, precision=HIGHEST, preferred_element_type=jnp.float32) - spatial_weight * (
        above + below + west + east
    )


def send_buffer(send_ref, values):
    lanes = lax.broadcasted_iota(jnp.int32, (1, send_ref.shape[1]), 1)
    row = jnp.zeros((1, send_ref.shape[1]), jnp.float32)
    for j, value in enumerate(values):
        row = row + jnp.where(lanes == j, jnp.sum(value, keepdims=True), 0.0)
    send_ref[...] = jnp.broadcast_to(row, send_ref.shape)


def first_kernel(k_ref, r_ref, ru_ref, rd_ref, rl_ref, rr_ref, w_ref, send_ref):
    r = r_ref[...]
    w = operate(k_ref[...], r, ru_ref[...], rd_ref[...], rl_ref[...], rr_ref[...])
    w_ref[...] = w
    send_buffer(send_ref, [r * r, r * w])


def second_kernel(got_ref, k_ref, r_ref, ru_ref, rd_ref, rl_ref, rr_ref, w_ref, wu_ref, wd_ref, wl_ref, wr_ref,
                  r_out, x_out, w_out, send_ref, scal_ref):
    sums = jnp.sum(got_ref[...], axis=0, keepdims=True)
    norm = lane_value(sums, 0)
    alpha = norm / lane_value(sums, 1)
    p = r_ref[...]
    q = w_ref[...]
    x_out[...] = alpha * p
    r = p - alpha * q
    r_out[...] = r
    halo = [h[...] - alpha * g[...] for h, g in zip((ru_ref, rd_ref, rl_ref, rr_ref), (wu_ref, wd_ref, wl_ref, wr_ref))]
    w = operate(k_ref[...], r, *halo)
    w_out[...] = w
    send_buffer(send_ref, [r * r, r * w, r * q, p * w, p * q])
    lanes = lax.broadcasted_iota(jnp.int32, scal_ref.shape, 1)
    scal_ref[...] = jnp.where(lanes == 0, norm, jnp.where(lanes == 1, alpha, 0.0))


def step_scalars(got_ref, scal_ref):
    sums = jnp.sum(got_ref[...], axis=0, keepdims=True)
    previous = scal_ref[...]
    norm = lane_value(sums, 0)
    beta = norm / lane_value(previous, 0)
    curvature = lane_value(sums, 1) + beta * (lane_value(sums, 2) + lane_value(sums, 3)) + beta * beta * lane_value(sums, 4)
    return norm, beta, norm / curvature


def third_kernel(got_ref, scal_ref, k_ref, r_ref, p_ref, q_ref, x_ref, w_ref,
                 ru_ref, rd_ref, rl_ref, rr_ref, qu_ref, qd_ref, ql_ref, qr_ref, wu_ref, wd_ref, wl_ref, wr_ref,
                 r_out, p_out, q_out, x_out, w_out, send_ref, scal_out):
    norm, beta, alpha = step_scalars(got_ref, scal_ref)
    alpha_first = lane_value(scal_ref[...], 1)
    p = r_ref[...] + beta * p_ref[...]
    q = w_ref[...] + beta * q_ref[...]
    p_out[...] = p
    q_out[...] = q
    x_out[...] = x_ref[...] + alpha * p
    r = r_ref[...] - alpha * q
    r_out[...] = r
    halo = []
    for h, k, g in zip((ru_ref, rd_ref, rl_ref, rr_ref), (qu_ref, qd_ref, ql_ref, qr_ref), (wu_ref, wd_ref, wl_ref, wr_ref)):
        halo.append((h[...] - alpha_first * k[...]) - alpha * (g[...] + beta * k[...]))
    w = operate(k_ref[...], r, *halo)
    w_out[...] = w
    send_buffer(send_ref, [r * r, r * w, r * q, p * w, p * q])
    lanes = lax.broadcasted_iota(jnp.int32, scal_out.shape, 1)
    scal_out[...] = jnp.where(lanes == 0, norm, jnp.where(lanes == 1, alpha, 0.0))


def last_kernel(got_ref, scal_ref, r_ref, p_ref, q_ref, x_ref, w_ref, x_out, r_out):
    norm, beta, alpha = step_scalars(got_ref, scal_ref)
    p = r_ref[...] + beta * p_ref[...]
    q = w_ref[...] + beta * q_ref[...]
    x_out[...] = x_ref[...] + alpha * p
    r_out[...] = r_ref[...] - alpha * q


def call(kernel, shapes, *args):
    return pl.pallas_call(kernel, out_shape=[jax.ShapeDtypeStruct(s, jnp.float32) for s in shapes])(*args)


def reduce_all(send):
    return lax.all_to_all(send, ("pair", "tile"), 0, 0, tiled=True)


def exchange_rows_cols(cells):
    return (
        from_prev(cells, "tile"),
        from_next(cells, "tile"),
        from_prev(cells[:, -1:], "pair"),
        from_next(cells[:, :1], "pair"),
    )


def body(phase, incidence, pair_weight):
    groups = lax.axis_size("pair")
    cols = phase.shape[2] // groups
    padded = jnp.pad(phase[:, 0, :], ((0, 0), (1, 1)))
    windows = jnp.stack([padded[:, j * cols : j * cols + cols + 2] for j in range(groups)])
    meta = jnp.stack(
        [incidence[:, 0].astype(jnp.float32), incidence[:, 1].astype(jnp.float32), pair_weight], axis=1
    )
    meta = jnp.pad(meta, ((0, 0), (0, 3)))
    chunks = jnp.concatenate([windows, jnp.broadcast_to(meta, (groups,) + meta.shape)], axis=2)
    got = lax.all_to_all(chunks, "pair", 0, 0, tiled=True).reshape(-1, chunks.shape[2])
    values = got[:, : cols + 2]
    earlier = got[:, cols + 2 : cols + 3]
    later = got[:, cols + 3 : cols + 4]
    weight = got[:, cols + 4 : cols + 5]
    dates = jnp.arange(DATES, dtype=jnp.float32)
    network = ((dates[None, :] == later).astype(jnp.float32) - (dates[None, :] == earlier).astype(jnp.float32)).astype(
        jnp.bfloat16
    )
    weighted = weight * values
    high = lax.reduce_precision(weighted, exponent_bits=8, mantissa_bits=7)
    rest = weighted - high
    middle = lax.reduce_precision(rest, exponent_bits=8, mantissa_bits=7)
    low = rest - middle
    high, middle, low = (part.astype(jnp.bfloat16) for part in (high, middle, low))
    width = values.shape[1]
    pieces = jnp.einsum(
        "kt,kc->tc", network, jnp.concatenate([high, middle, low], axis=1), preferred_element_type=jnp.float32
    )
    right_wide = pieces[:, :width] + pieces[:, width : 2 * width] + pieces[:, 2 * width :]
    span_hot = (jnp.arange(SPAN, dtype=jnp.float32)[None, :] == (later - earlier)).astype(jnp.float32)
    start_hot = (dates[None, :] == earlier).astype(jnp.float32)
    span_weights = jnp.einsum("kt,kd->td", start_hot, span_hot * weight, precision=HIGHEST)
    matrix = normal_matrix(span_weights)
    residual = right_wide[:, 1:-1]
    residual_halo = (
        from_prev(residual, "tile"),
        from_next(residual, "tile"),
        right_wide[:, :1],
        right_wide[:, -1:],
    )
    count = lax.axis_size("pair") * lax.axis_size("tile")
    field = residual.shape
    lanes = 128
    send_shape = (count, lanes)
    w0, send = call(first_kernel, [field, send_shape], matrix, residual, *residual_halo)
    w0_halo = exchange_rows_cols(w0)
    got = reduce_all(send)
    r1, x1, w1, send, scal = call(
        second_kernel, [field, field, field, send_shape, (1, lanes)], got, matrix, residual, *residual_halo, w0, *w0_halo
    )
    w1_halo = exchange_rows_cols(w1)
    got = reduce_all(send)
    r2, p1, q1, x2, w2, send, scal = call(
        third_kernel,
        [field, field, field, field, field, send_shape, (1, lanes)],
        got, scal, matrix, r1, residual, w0, x1, w1, *residual_halo, *w0_halo, *w1_halo,
    )
    got = reduce_all(send)
    solution_field, residual = call(last_kernel, [field, field], got, scal, r2, p1, q1, x2, w2)
    return (solution_field[:, None, :], residual[:, None, :])


def solution(mesh):
    return jax.shard_map(
        body,
        mesh=mesh,
        in_specs=(P("pair", "tile", None), P("pair", None), P("pair")),
        out_specs=(P(None, "tile", "pair"), P(None, "tile", "pair")),
        check_vma=False,
    )
```

```python
import numpy as np
import jax
import jax.numpy as jnp
from jax import lax
from jax.sharding import PartitionSpec as P
from jax.experimental import pallas as pl
from jax.experimental.pallas import tpu as pltpu

DATES = 400
ITERS = 3
SPAN = 8

temporal_weight = 2.0
spatial_weight = 0.5
ridge_weight = 0.05

HIGHEST = lax.Precision.HIGHEST


def temporal_matrix():
    second = np.zeros((DATES - 2, DATES), np.float64)
    rows = np.arange(DATES - 2)
    second[rows, rows] = 1.0
    second[rows, rows + 1] = -2.0
    second[rows, rows + 2] = 1.0
    return (second.T @ second).astype(np.float32)


def from_prev(cells, axis):
    count = lax.axis_size(axis)
    return lax.ppermute(cells, axis, [(i, i + 1) for i in range(count - 1)])


def from_next(cells, axis):
    count = lax.axis_size(axis)
    return lax.ppermute(cells, axis, [(i + 1, i) for i in range(count - 1)])


def exchange(cells):
    return (
        from_prev(cells, "tile"),
        from_next(cells, "tile"),
        from_prev(cells[:, -1:], "pair"),
        from_next(cells[:, :1], "pair"),
    )


def neighbours(cells, halo):
    above, below, left, right = halo
    west = jnp.concatenate([left, cells[:, :-1]], axis=1)
    east = jnp.concatenate([cells[:, 1:], right], axis=1)
    return above + below + west + east


def apply_operator(matrix, cells, halo):
    return jnp.dot(matrix, cells, precision=HIGHEST) - spatial_weight * neighbours(cells, halo)


def total(parts):
    count = lax.axis_size("pair") * lax.axis_size("tile")
    sent = jnp.broadcast_to(parts[None, :], (count, parts.shape[0]))
    got = lax.all_to_all(sent, ("pair", "tile"), 0, 0, tiled=True)
    return jnp.sum(got, axis=0)


def normal_matrix(weights):
    dates = jnp.arange(DATES, dtype=jnp.int32)
    offset = dates[None, :] - dates[:, None]
    upper = jnp.zeros((DATES, DATES), jnp.float32)
    for d in range(1, SPAN):
        upper = upper + jnp.where(offset == d, -weights[:, d : d + 1], 0.0)
    coupling = upper + upper.T
    degree = -jnp.sum(coupling, axis=1)
    diagonal = degree + (4.0 * spatial_weight + ridge_weight)
    return coupling + jnp.where(offset == 0, diagonal[:, None], 0.0) + temporal_weight * temporal_matrix()


def lane_value(vector, j):
    lanes = lax.broadcasted_iota(jnp.int32, vector.shape, 1)
    return jnp.sum(jnp.where(lanes == j, vector, 0.0), axis=1, keepdims=True)


def shifted(cells, left, right):
    width = cells.shape[1]
    lanes = lax.broadcasted_iota(jnp.int32, cells.shape, 1)
    probe = pltpu.roll(lanes, 1, 1)
    forward = probe == jnp.where(lanes == 0, width - 1, lanes - 1)
    one = pltpu.roll(cells, 1, 1)
    back = pltpu.roll(cells, width - 1, 1)
    west = jnp.where(lanes == 0, left, jnp.where(forward, one, back))
    east = jnp.where(lanes == width - 1, right, jnp.where(forward, back, one))
    return west, east


def operate(matrix, cells, above, below, left, right):
    west, east = shifted(cells, left, right)
    return jnp.dot(matrix, cells, precision=HIGHEST, preferred_element_type=jnp.float32) - spatial_weight * (
        above + below + west + east
    )


def send_buffer(send_ref, values):
    lanes = lax.broadcasted_iota(jnp.int32, (1, send_ref.shape[1]), 1)
    row = jnp.zeros((1, send_ref.shape[1]), jnp.float32)
    for j, value in enumerate(values):
        row = row + jnp.where(lanes == j, jnp.sum(value, keepdims=True), 0.0)
    send_ref[...] = jnp.broadcast_to(row, send_ref.shape)


def first_kernel(k_ref, r_ref, ru_ref, rd_ref, rl_ref, rr_ref, w_ref, send_ref):
    r = r_ref[...]
    w = operate(k_ref[...], r, ru_ref[...], rd_ref[...], rl_ref[...], rr_ref[...])
    w_ref[...] = w
    send_buffer(send_ref, [r * r, r * w])


def second_kernel(got_ref, k_ref, r_ref, ru_ref, rd_ref, rl_ref, rr_ref, w_ref, wu_ref, wd_ref, wl_ref, wr_ref,
                  r_out, x_out, w_out, send_ref, scal_ref):
    sums = jnp.sum(got_ref[...], axis=0, keepdims=True)
    norm = lane_value(sums, 0)
    alpha = norm / lane_value(sums, 1)
    p = r_ref[...]
    q = w_ref[...]
    x_out[...] = alpha * p
    r = p - alpha * q
    r_out[...] = r
    halo = [h[...] - alpha * g[...] for h, g in zip((ru_ref, rd_ref, rl_ref, rr_ref), (wu_ref, wd_ref, wl_ref, wr_ref))]
    w = operate(k_ref[...], r, *halo)
    w_out[...] = w
    send_buffer(send_ref, [r * r, r * w, r * q, p * w, p * q])
    lanes = lax.broadcasted_iota(jnp.int32, scal_ref.shape, 1)
    scal_ref[...] = jnp.where(lanes == 0, norm, jnp.where(lanes == 1, alpha, 0.0))


def step_scalars(got_ref, scal_ref):
    sums = jnp.sum(got_ref[...], axis=0, keepdims=True)
    previous = scal_ref[...]
    norm = lane_value(sums, 0)
    beta = norm / lane_value(previous, 0)
    curvature = lane_value(sums, 1) + beta * (lane_value(sums, 2) + lane_value(sums, 3)) + beta * beta * lane_value(sums, 4)
    return norm, beta, norm / curvature


def third_kernel(got_ref, scal_ref, k_ref, r_ref, p_ref, q_ref, x_ref, w_ref,
                 ru_ref, rd_ref, rl_ref, rr_ref, qu_ref, qd_ref, ql_ref, qr_ref, wu_ref, wd_ref, wl_ref, wr_ref,
                 r_out, p_out, q_out, x_out, w_out, send_ref, scal_out):
    norm, beta, alpha = step_scalars(got_ref, scal_ref)
    alpha_first = lane_value(scal_ref[...], 1)
    p = r_ref[...] + beta * p_ref[...]
    q = w_ref[...] + beta * q_ref[...]
    p_out[...] = p
    q_out[...] = q
    x_out[...] = x_ref[...] + alpha * p
    r = r_ref[...] - alpha * q
    r_out[...] = r
    halo = []
    for h, k, g in zip((ru_ref, rd_ref, rl_ref, rr_ref), (qu_ref, qd_ref, ql_ref, qr_ref), (wu_ref, wd_ref, wl_ref, wr_ref)):
        halo.append((h[...] - alpha_first * k[...]) - alpha * (g[...] + beta * k[...]))
    w = operate(k_ref[...], r, *halo)
    w_out[...] = w
    send_buffer(send_ref, [r * r, r * w, r * q, p * w, p * q])
    lanes = lax.broadcasted_iota(jnp.int32, scal_out.shape, 1)
    scal_out[...] = jnp.where(lanes == 0, norm, jnp.where(lanes == 1, alpha, 0.0))


def last_kernel(got_ref, scal_ref, r_ref, p_ref, q_ref, x_ref, w_ref, x_out, r_out):
    norm, beta, alpha = step_scalars(got_ref, scal_ref)
    p = r_ref[...] + beta * p_ref[...]
    q = w_ref[...] + beta * q_ref[...]
    x_out[...] = x_ref[...] + alpha * p
    r_out[...] = r_ref[...] - alpha * q


def call(kernel, shapes, *args):
    resident = pl.BlockSpec(memory_space=pltpu.VMEM)
    return pl.pallas_call(
        kernel,
        out_shape=[jax.ShapeDtypeStruct(s, jnp.float32) for s in shapes],
        in_specs=[resident] * len(args),
        out_specs=[resident] * len(shapes),
    )(*args)


def reduce_all(send):
    return lax.all_to_all(send, ("pair", "tile"), 0, 0, tiled=True)


def exchange_rows_cols(cells):
    return (
        from_prev(cells, "tile"),
        from_next(cells, "tile"),
        from_prev(cells[:, -1:], "pair"),
        from_next(cells[:, :1], "pair"),
    )


def body(phase, incidence, pair_weight):
    groups = lax.axis_size("pair")
    cols = phase.shape[2] // groups
    padded = jnp.pad(phase[:, 0, :], ((0, 0), (1, 1)))
    windows = jnp.stack([padded[:, j * cols : j * cols + cols + 2] for j in range(groups)])
    meta = jnp.stack(
        [incidence[:, 0].astype(jnp.float32), incidence[:, 1].astype(jnp.float32), pair_weight], axis=1
    )
    meta = jnp.pad(meta, ((0, 0), (0, 3)))
    chunks = jnp.concatenate([windows, jnp.broadcast_to(meta, (groups,) + meta.shape)], axis=2)
    got = lax.all_to_all(chunks, "pair", 0, 0, tiled=True).reshape(-1, chunks.shape[2])
    values = got[:, : cols + 2]
    earlier = got[:, cols + 2 : cols + 3]
    later = got[:, cols + 3 : cols + 4]
    weight = got[:, cols + 4 : cols + 5]
    dates = jnp.arange(DATES, dtype=jnp.float32)
    network = ((dates[None, :] == later).astype(jnp.float32) - (dates[None, :] == earlier).astype(jnp.float32)).astype(
        jnp.bfloat16
    )
    weighted = weight * values
    high = lax.reduce_precision(weighted, exponent_bits=8, mantissa_bits=7)
    rest = weighted - high
    middle = lax.reduce_precision(rest, exponent_bits=8, mantissa_bits=7)
    low = rest - middle
    high, middle, low = (part.astype(jnp.bfloat16) for part in (high, middle, low))
    width = values.shape[1]
    pieces = jnp.einsum(
        "kt,kc->tc", network, jnp.concatenate([high, middle, low], axis=1), preferred_element_type=jnp.float32
    )
    right_wide = pieces[:, :width] + pieces[:, width : 2 * width] + pieces[:, 2 * width :]
    span_hot = (jnp.arange(SPAN, dtype=jnp.float32)[None, :] == (later - earlier)).astype(jnp.float32)
    start_hot = (dates[None, :] == earlier).astype(jnp.float32)
    span_weights = jnp.einsum("kt,kd->td", start_hot, span_hot * weight, precision=HIGHEST)
    matrix = normal_matrix(span_weights)
    residual = right_wide[:, 1:-1]
    residual_halo = (
        from_prev(residual, "tile"),
        from_next(residual, "tile"),
        right_wide[:, :1],
        right_wide[:, -1:],
    )
    count = lax.axis_size("pair") * lax.axis_size("tile")
    field = residual.shape
    lanes = 128
    send_shape = (count, lanes)
    w0, send = call(first_kernel, [field, send_shape], matrix, residual, *residual_halo)
    w0_halo = exchange_rows_cols(w0)
    got = reduce_all(send)
    r1, x1, w1, send, scal = call(
        second_kernel, [field, field, field, send_shape, (1, lanes)], got, matrix, residual, *residual_halo, w0, *w0_halo
    )
    w1_halo = exchange_rows_cols(w1)
    got = reduce_all(send)
    r2, p1, q1, x2, w2, send, scal = call(
        third_kernel,
        [field, field, field, field, field, send_shape, (1, lanes)],
        got, scal, matrix, r1, residual, w0, x1, w1, *residual_halo, *w0_halo, *w1_halo,
    )
    got = reduce_all(send)
    solution_field, residual = call(last_kernel, [field, field], got, scal, r2, p1, q1, x2, w2)
    return (solution_field[:, None, :], residual[:, None, :])


def solution(mesh):
    return jax.shard_map(
        body,
        mesh=mesh,
        in_specs=(P("pair", "tile", None), P("pair", None), P("pair")),
        out_specs=(P(None, "tile", "pair"), P(None, "tile", "pair")),
        check_vma=False,
    )
```

```python
import numpy as np
import jax
import jax.numpy as jnp
from jax import lax
from jax.sharding import PartitionSpec as P
from jax.experimental import pallas as pl
from jax.experimental.pallas import tpu as pltpu

DATES = 400
ITERS = 3
SPAN = 8

temporal_weight = 2.0
spatial_weight = 0.5
ridge_weight = 0.05

HIGHEST = lax.Precision.HIGHEST


def temporal_matrix():
    second = np.zeros((DATES - 2, DATES), np.float64)
    rows = np.arange(DATES - 2)
    second[rows, rows] = 1.0
    second[rows, rows + 1] = -2.0
    second[rows, rows + 2] = 1.0
    return (second.T @ second).astype(np.float32)


def from_prev(cells, axis):
    count = lax.axis_size(axis)
    return lax.ppermute(cells, axis, [(i, i + 1) for i in range(count - 1)])


def from_next(cells, axis):
    count = lax.axis_size(axis)
    return lax.ppermute(cells, axis, [(i + 1, i) for i in range(count - 1)])


def exchange(cells):
    return (
        from_prev(cells, "tile"),
        from_next(cells, "tile"),
        from_prev(cells[:, -1:], "pair"),
        from_next(cells[:, :1], "pair"),
    )


def neighbours(cells, halo):
    above, below, left, right = halo
    west = jnp.concatenate([left, cells[:, :-1]], axis=1)
    east = jnp.concatenate([cells[:, 1:], right], axis=1)
    return above + below + west + east


def apply_operator(matrix, cells, halo):
    return jnp.dot(matrix, cells, precision=HIGHEST) - spatial_weight * neighbours(cells, halo)


def total(parts):
    count = lax.axis_size("pair") * lax.axis_size("tile")
    sent = jnp.broadcast_to(parts[None, :], (count, parts.shape[0]))
    got = lax.all_to_all(sent, ("pair", "tile"), 0, 0, tiled=True)
    return jnp.sum(got, axis=0)


def regularizer_matrix():
    return temporal_weight * temporal_matrix() + (4.0 * spatial_weight + ridge_weight) * np.eye(DATES, dtype=np.float32)


def lane_value(vector, j):
    lanes = lax.broadcasted_iota(jnp.int32, vector.shape, 1)
    return jnp.sum(jnp.where(lanes == j, vector, 0.0), axis=1, keepdims=True)


def shifted(cells, left, right):
    width = cells.shape[1]
    lanes = lax.broadcasted_iota(jnp.int32, cells.shape, 1)
    probe = pltpu.roll(lanes, 1, 1)
    forward = probe == jnp.where(lanes == 0, width - 1, lanes - 1)
    one = pltpu.roll(cells, 1, 1)
    back = pltpu.roll(cells, width - 1, 1)
    west = jnp.where(lanes == 0, left, jnp.where(forward, one, back))
    east = jnp.where(lanes == width - 1, right, jnp.where(forward, back, one))
    return west, east


def operate(matrix, cells, above, below, left, right):
    west, east = shifted(cells, left, right)
    return jnp.dot(matrix, cells, precision=HIGHEST, preferred_element_type=jnp.float32) - spatial_weight * (
        above + below + west + east
    )


def send_buffer(send_ref, values):
    lanes = lax.broadcasted_iota(jnp.int32, (1, send_ref.shape[1]), 1)
    row = jnp.zeros((1, send_ref.shape[1]), jnp.float32)
    for j, value in enumerate(values):
        row = row + jnp.where(lanes == j, jnp.sum(value, keepdims=True), 0.0)
    send_ref[...] = jnp.broadcast_to(row, send_ref.shape)


def first_kernel(k_ref, r_ref, ru_ref, rd_ref, rl_ref, rr_ref, w_ref, send_ref):
    r = r_ref[...]
    w = operate(k_ref[...], r, ru_ref[...], rd_ref[...], rl_ref[...], rr_ref[...])
    w_ref[...] = w
    send_buffer(send_ref, [r * r, r * w])


def second_kernel(got_ref, k_ref, r_ref, ru_ref, rd_ref, rl_ref, rr_ref, w_ref, wu_ref, wd_ref, wl_ref, wr_ref,
                  r_out, x_out, w_out, send_ref, scal_ref):
    sums = jnp.sum(got_ref[...], axis=0, keepdims=True)
    norm = lane_value(sums, 0)
    alpha = norm / lane_value(sums, 1)
    p = r_ref[...]
    q = w_ref[...]
    x_out[...] = alpha * p
    r = p - alpha * q
    r_out[...] = r
    halo = [h[...] - alpha * g[...] for h, g in zip((ru_ref, rd_ref, rl_ref, rr_ref), (wu_ref, wd_ref, wl_ref, wr_ref))]
    w = operate(k_ref[...], r, *halo)
    w_out[...] = w
    send_buffer(send_ref, [r * r, r * w, r * q, p * w, p * q])
    lanes = lax.broadcasted_iota(jnp.int32, scal_ref.shape, 1)
    scal_ref[...] = jnp.where(lanes == 0, norm, jnp.where(lanes == 1, alpha, 0.0))


def step_scalars(got_ref, scal_ref):
    sums = jnp.sum(got_ref[...], axis=0, keepdims=True)
    previous = scal_ref[...]
    norm = lane_value(sums, 0)
    beta = norm / lane_value(previous, 0)
    curvature = lane_value(sums, 1) + beta * (lane_value(sums, 2) + lane_value(sums, 3)) + beta * beta * lane_value(sums, 4)
    return norm, beta, norm / curvature


def third_kernel(got_ref, scal_ref, k_ref, r_ref, p_ref, q_ref, x_ref, w_ref,
                 ru_ref, rd_ref, rl_ref, rr_ref, qu_ref, qd_ref, ql_ref, qr_ref, wu_ref, wd_ref, wl_ref, wr_ref,
                 r_out, p_out, q_out, x_out, w_out, send_ref, scal_out):
    norm, beta, alpha = step_scalars(got_ref, scal_ref)
    alpha_first = lane_value(scal_ref[...], 1)
    p = r_ref[...] + beta * p_ref[...]
    q = w_ref[...] + beta * q_ref[...]
    p_out[...] = p
    q_out[...] = q
    x_out[...] = x_ref[...] + alpha * p
    r = r_ref[...] - alpha * q
    r_out[...] = r
    halo = []
    for h, k, g in zip((ru_ref, rd_ref, rl_ref, rr_ref), (qu_ref, qd_ref, ql_ref, qr_ref), (wu_ref, wd_ref, wl_ref, wr_ref)):
        halo.append((h[...] - alpha_first * k[...]) - alpha * (g[...] + beta * k[...]))
    w = operate(k_ref[...], r, *halo)
    w_out[...] = w
    send_buffer(send_ref, [r * r, r * w, r * q, p * w, p * q])
    lanes = lax.broadcasted_iota(jnp.int32, scal_out.shape, 1)
    scal_out[...] = jnp.where(lanes == 0, norm, jnp.where(lanes == 1, alpha, 0.0))


def last_kernel(got_ref, scal_ref, r_ref, p_ref, q_ref, x_ref, w_ref, x_out, r_out):
    norm, beta, alpha = step_scalars(got_ref, scal_ref)
    p = r_ref[...] + beta * p_ref[...]
    q = w_ref[...] + beta * q_ref[...]
    x_out[...] = x_ref[...] + alpha * p
    r_out[...] = r_ref[...] - alpha * q


def call(kernel, shapes, *args):
    resident = pl.BlockSpec(memory_space=pltpu.VMEM)
    return pl.pallas_call(
        kernel,
        out_shape=[jax.ShapeDtypeStruct(s, jnp.float32) for s in shapes],
        in_specs=[resident] * len(args),
        out_specs=[resident] * len(shapes),
    )(*args)


def reduce_all(send):
    return lax.all_to_all(send, ("pair", "tile"), 0, 0, tiled=True)


def exchange_rows_cols(cells):
    return (
        from_prev(cells, "tile"),
        from_next(cells, "tile"),
        from_prev(cells[:, -1:], "pair"),
        from_next(cells[:, :1], "pair"),
    )


def body(phase, incidence, pair_weight):
    groups = lax.axis_size("pair")
    cols = phase.shape[2] // groups
    padded = jnp.pad(phase[:, 0, :], ((0, 0), (1, 1)))
    windows = jnp.stack([padded[:, j * cols : j * cols + cols + 2] for j in range(groups)])
    meta = jnp.stack(
        [incidence[:, 0].astype(jnp.float32), incidence[:, 1].astype(jnp.float32), pair_weight], axis=1
    )
    meta = jnp.pad(meta, ((0, 0), (0, 3)))
    chunks = jnp.concatenate([windows, jnp.broadcast_to(meta, (groups,) + meta.shape)], axis=2)
    got = lax.all_to_all(chunks, "pair", 0, 0, tiled=True).reshape(-1, chunks.shape[2])
    values = got[:, : cols + 2]
    earlier = got[:, cols + 2 : cols + 3]
    later = got[:, cols + 3 : cols + 4]
    weight = got[:, cols + 4 : cols + 5]
    dates = jnp.arange(DATES, dtype=jnp.float32)
    network = ((dates[None, :] == later).astype(jnp.float32) - (dates[None, :] == earlier).astype(jnp.float32)).astype(
        jnp.bfloat16
    )
    width = values.shape[1]
    operand = jnp.concatenate([weight * values, weight * network.astype(jnp.float32)], axis=1)
    high = lax.reduce_precision(operand, exponent_bits=8, mantissa_bits=7)
    rest = operand - high
    middle = lax.reduce_precision(rest, exponent_bits=8, mantissa_bits=7)
    low = rest - middle
    parts = jnp.concatenate([p.astype(jnp.bfloat16) for p in (high, middle, low)], axis=1)
    pieces = jnp.einsum("kt,kc->tc", network, parts, preferred_element_type=jnp.float32)
    span = width + DATES
    summed = pieces[:, :span] + pieces[:, span : 2 * span] + pieces[:, 2 * span :]
    right_wide = summed[:, :width]
    matrix = summed[:, width:] + regularizer_matrix()
    residual = right_wide[:, 1:-1]
    residual_halo = (
        from_prev(residual, "tile"),
        from_next(residual, "tile"),
        right_wide[:, :1],
        right_wide[:, -1:],
    )
    count = lax.axis_size("pair") * lax.axis_size("tile")
    field = residual.shape
    lanes = 128
    send_shape = (count, lanes)
    w0, send = call(first_kernel, [field, send_shape], matrix, residual, *residual_halo)
    w0_halo = exchange_rows_cols(w0)
    got = reduce_all(send)
    r1, x1, w1, send, scal = call(
        second_kernel, [field, field, field, send_shape, (1, lanes)], got, matrix, residual, *residual_halo, w0, *w0_halo
    )
    w1_halo = exchange_rows_cols(w1)
    got = reduce_all(send)
    r2, p1, q1, x2, w2, send, scal = call(
        third_kernel,
        [field, field, field, field, field, send_shape, (1, lanes)],
        got, scal, matrix, r1, residual, w0, x1, w1, *residual_halo, *w0_halo, *w1_halo,
    )
    got = reduce_all(send)
    solution_field, residual = call(last_kernel, [field, field], got, scal, r2, p1, q1, x2, w2)
    return (solution_field[:, None, :], residual[:, None, :])


def solution(mesh):
    return jax.shard_map(
        body,
        mesh=mesh,
        in_specs=(P("pair", "tile", None), P("pair", None), P("pair")),
        out_specs=(P(None, "tile", "pair"), P(None, "tile", "pair")),
        check_vma=False,
    )
```

```python
import numpy as np
import jax
import jax.numpy as jnp
from jax import lax
from jax.sharding import PartitionSpec as P
from jax.experimental import pallas as pl
from jax.experimental.pallas import tpu as pltpu

DATES = 400
ITERS = 3
SPAN = 8

temporal_weight = 2.0
spatial_weight = 0.5
ridge_weight = 0.05

HIGHEST = lax.Precision.HIGHEST


def temporal_matrix():
    second = np.zeros((DATES - 2, DATES), np.float64)
    rows = np.arange(DATES - 2)
    second[rows, rows] = 1.0
    second[rows, rows + 1] = -2.0
    second[rows, rows + 2] = 1.0
    return (second.T @ second).astype(np.float32)


def from_prev(cells, axis):
    count = lax.axis_size(axis)
    return lax.ppermute(cells, axis, [(i, i + 1) for i in range(count - 1)])


def from_next(cells, axis):
    count = lax.axis_size(axis)
    return lax.ppermute(cells, axis, [(i + 1, i) for i in range(count - 1)])


def exchange(cells):
    return (
        from_prev(cells, "tile"),
        from_next(cells, "tile"),
        from_prev(cells[:, -1:], "pair"),
        from_next(cells[:, :1], "pair"),
    )


def neighbours(cells, halo):
    above, below, left, right = halo
    west = jnp.concatenate([left, cells[:, :-1]], axis=1)
    east = jnp.concatenate([cells[:, 1:], right], axis=1)
    return above + below + west + east


def apply_operator(matrix, cells, halo):
    return jnp.dot(matrix, cells, precision=HIGHEST) - spatial_weight * neighbours(cells, halo)


def total(parts):
    count = lax.axis_size("pair") * lax.axis_size("tile")
    sent = jnp.broadcast_to(parts[None, :], (count, parts.shape[0]))
    got = lax.all_to_all(sent, ("pair", "tile"), 0, 0, tiled=True)
    return jnp.sum(got, axis=0)


def normal_matrix(weights):
    dates = jnp.arange(DATES, dtype=jnp.int32)
    offset = dates[None, :] - dates[:, None]
    upper = jnp.zeros((DATES, DATES), jnp.float32)
    for d in range(1, SPAN):
        upper = upper + jnp.where(offset == d, -weights[:, d : d + 1], 0.0)
    coupling = upper + upper.T
    degree = -jnp.sum(coupling, axis=1)
    diagonal = degree + (4.0 * spatial_weight + ridge_weight)
    return coupling + jnp.where(offset == 0, diagonal[:, None], 0.0) + temporal_weight * temporal_matrix()


def lane_value(vector, j):
    lanes = lax.broadcasted_iota(jnp.int32, vector.shape, 1)
    return jnp.sum(jnp.where(lanes == j, vector, 0.0), axis=1, keepdims=True)


def shifted(cells, left, right):
    width = cells.shape[1]
    lanes = lax.broadcasted_iota(jnp.int32, cells.shape, 1)
    probe = pltpu.roll(lanes, 1, 1)
    forward = probe == jnp.where(lanes == 0, width - 1, lanes - 1)
    one = pltpu.roll(cells, 1, 1)
    back = pltpu.roll(cells, width - 1, 1)
    west = jnp.where(lanes == 0, left, jnp.where(forward, one, back))
    east = jnp.where(lanes == width - 1, right, jnp.where(forward, back, one))
    return west, east


def operate(matrix, cells, above, below, left, right):
    west, east = shifted(cells, left, right)
    return jnp.dot(matrix, cells, precision=HIGHEST, preferred_element_type=jnp.float32) - spatial_weight * (
        above + below + west + east
    )


def send_buffer(send_ref, values):
    lanes = lax.broadcasted_iota(jnp.int32, (1, send_ref.shape[1]), 1)
    row = jnp.zeros((1, send_ref.shape[1]), jnp.float32)
    for j, value in enumerate(values):
        row = row + jnp.where(lanes == j, jnp.sum(value, keepdims=True), 0.0)
    send_ref[...] = jnp.broadcast_to(row, send_ref.shape)


def image_kernel(k_ref, v_ref, vu_ref, vd_ref, vl_ref, vr_ref, w_out):
    w_out[...] = operate(k_ref[...], v_ref[...], vu_ref[...], vd_ref[...], vl_ref[...], vr_ref[...])


def gram_kernel(k_ref, r_ref, w_ref, wu_ref, wd_ref, wl_ref, wr_ref, z_out, send_ref):
    r = r_ref[...]
    w = w_ref[...]
    z = operate(k_ref[...], w, wu_ref[...], wd_ref[...], wl_ref[...], wr_ref[...])
    z_out[...] = z
    send_buffer(send_ref, [r * r, r * w, w * w, r * z, w * z])


def block_kernel(got_ref, k_ref, r_ref, w_ref, z_ref, ru_ref, rd_ref, rl_ref, rr_ref, wu_ref, wd_ref, wl_ref, wr_ref,
                 zu_ref, zd_ref, zl_ref, zr_ref, r_out, p_out, q_out, x_out, w_out, send_ref, scal_out):
    sums = jnp.sum(got_ref[...], axis=0, keepdims=True)
    norm_first = lane_value(sums, 0)
    curvature_first = lane_value(sums, 1)
    alpha_first = norm_first / curvature_first
    norm = norm_first - 2.0 * alpha_first * curvature_first + alpha_first * alpha_first * lane_value(sums, 2)
    beta = norm / norm_first
    a = 1.0 + beta
    b = -alpha_first
    curvature = a * a * curvature_first + a * b * (lane_value(sums, 3) + lane_value(sums, 2)) + b * b * lane_value(sums, 4)
    alpha = norm / curvature
    r0 = r_ref[...]
    w0 = w_ref[...]
    z0 = z_ref[...]
    p = a * r0 + b * w0
    q = a * w0 + b * z0
    p_out[...] = p
    q_out[...] = q
    x_out[...] = alpha_first * r0 + alpha * p
    r = (r0 - alpha_first * w0) - alpha * q
    r_out[...] = r
    halo = []
    for hr, hw, hz in zip((ru_ref, rd_ref, rl_ref, rr_ref), (wu_ref, wd_ref, wl_ref, wr_ref), (zu_ref, zd_ref, zl_ref, zr_ref)):
        halo.append((hr[...] - alpha_first * hw[...]) - alpha * (a * hw[...] + b * hz[...]))
    w = operate(k_ref[...], r, *halo)
    w_out[...] = w
    send_buffer(send_ref, [r * r, r * w, r * q, p * w, p * q])
    lanes = lax.broadcasted_iota(jnp.int32, scal_out.shape, 1)
    scal_out[...] = jnp.where(lanes == 0, norm, 0.0)


def step_scalars(got_ref, scal_ref):
    sums = jnp.sum(got_ref[...], axis=0, keepdims=True)
    previous = scal_ref[...]
    norm = lane_value(sums, 0)
    beta = norm / lane_value(previous, 0)
    curvature = lane_value(sums, 1) + beta * (lane_value(sums, 2) + lane_value(sums, 3)) + beta * beta * lane_value(sums, 4)
    return norm, beta, norm / curvature


def last_kernel(got_ref, scal_ref, r_ref, p_ref, q_ref, x_ref, w_ref, x_out, r_out):
    norm, beta, alpha = step_scalars(got_ref, scal_ref)
    p = r_ref[...] + beta * p_ref[...]
    q = w_ref[...] + beta * q_ref[...]
    x_out[...] = x_ref[...] + alpha * p
    r_out[...] = r_ref[...] - alpha * q


def call(kernel, shapes, *args):
    resident = pl.BlockSpec(memory_space=pltpu.VMEM)
    return pl.pallas_call(
        kernel,
        out_shape=[jax.ShapeDtypeStruct(s, jnp.float32) for s in shapes],
        in_specs=[resident] * len(args),
        out_specs=[resident] * len(shapes),
    )(*args)


def reduce_all(send):
    return lax.all_to_all(send, ("pair", "tile"), 0, 0, tiled=True)


def exchange_rows_cols(cells):
    return (
        from_prev(cells, "tile"),
        from_next(cells, "tile"),
        from_prev(cells[:, -1:], "pair"),
        from_next(cells[:, :1], "pair"),
    )


def body(phase, incidence, pair_weight):
    groups = lax.axis_size("pair")
    cols = phase.shape[2] // groups
    padded = jnp.pad(phase[:, 0, :], ((0, 0), (1, 1)))
    windows = jnp.stack([padded[:, j * cols : j * cols + cols + 2] for j in range(groups)])
    meta = jnp.stack(
        [incidence[:, 0].astype(jnp.float32), incidence[:, 1].astype(jnp.float32), pair_weight], axis=1
    )
    meta = jnp.pad(meta, ((0, 0), (0, 3)))
    chunks = jnp.concatenate([windows, jnp.broadcast_to(meta, (groups,) + meta.shape)], axis=2)
    got = lax.all_to_all(chunks, "pair", 0, 0, tiled=True).reshape(-1, chunks.shape[2])
    values = got[:, : cols + 2]
    earlier = got[:, cols + 2 : cols + 3]
    later = got[:, cols + 3 : cols + 4]
    weight = got[:, cols + 4 : cols + 5]
    dates = jnp.arange(DATES, dtype=jnp.float32)
    network = ((dates[None, :] == later).astype(jnp.float32) - (dates[None, :] == earlier).astype(jnp.float32)).astype(
        jnp.bfloat16
    )
    weighted = weight * values
    high = lax.reduce_precision(weighted, exponent_bits=8, mantissa_bits=7)
    rest = weighted - high
    middle = lax.reduce_precision(rest, exponent_bits=8, mantissa_bits=7)
    low = rest - middle
    high, middle, low = (part.astype(jnp.bfloat16) for part in (high, middle, low))
    width = values.shape[1]
    pieces = jnp.einsum(
        "kt,kc->tc", network, jnp.concatenate([high, middle, low], axis=1), preferred_element_type=jnp.float32
    )
    right_wide = pieces[:, :width] + pieces[:, width : 2 * width] + pieces[:, 2 * width :]
    span_hot = (jnp.arange(SPAN, dtype=jnp.float32)[None, :] == (later - earlier)).astype(jnp.float32)
    start_hot = (dates[None, :] == earlier).astype(jnp.float32)
    span_weights = jnp.einsum("kt,kd->td", start_hot, span_hot * weight, precision=HIGHEST)
    matrix = normal_matrix(span_weights)
    residual = right_wide[:, 1:-1]
    residual_halo = (
        from_prev(residual, "tile"),
        from_next(residual, "tile"),
        right_wide[:, :1],
        right_wide[:, -1:],
    )
    count = lax.axis_size("pair") * lax.axis_size("tile")
    field = residual.shape
    lanes = 128
    send_shape = (count, lanes)
    (w0,) = call(image_kernel, [field], matrix, residual, *residual_halo)
    w0_halo = exchange_rows_cols(w0)
    z0, send = call(gram_kernel, [field, send_shape], matrix, residual, w0, *w0_halo)
    got = reduce_all(send)
    z0_halo = exchange_rows_cols(z0)
    r2, p1, q1, x2, w2, send, scal = call(
        block_kernel,
        [field, field, field, field, field, send_shape, (1, lanes)],
        got, matrix, residual, w0, z0, *residual_halo, *w0_halo, *z0_halo,
    )
    got = reduce_all(send)
    solution_field, residual = call(last_kernel, [field, field], got, scal, r2, p1, q1, x2, w2)
    return (solution_field[:, None, :], residual[:, None, :])


def solution(mesh):
    return jax.shard_map(
        body,
        mesh=mesh,
        in_specs=(P("pair", "tile", None), P("pair", None), P("pair")),
        out_specs=(P(None, "tile", "pair"), P(None, "tile", "pair")),
        check_vma=False,
    )
```

```python
import numpy as np
import jax
import jax.numpy as jnp
from jax import lax
from jax.sharding import PartitionSpec as P
from jax.experimental import pallas as pl
from jax.experimental.pallas import tpu as pltpu

DATES = 400
ITERS = 3
SPAN = 8
GRAM_PAIRS = ((0, 0), (0, 1), (0, 2), (0, 3), (1, 1), (1, 2), (1, 3), (2, 2), (2, 3))

temporal_weight = 2.0
spatial_weight = 0.5
ridge_weight = 0.05

HIGHEST = lax.Precision.HIGHEST


def temporal_matrix():
    second = np.zeros((DATES - 2, DATES), np.float64)
    rows = np.arange(DATES - 2)
    second[rows, rows] = 1.0
    second[rows, rows + 1] = -2.0
    second[rows, rows + 2] = 1.0
    return (second.T @ second).astype(np.float32)


def from_prev(cells, axis):
    count = lax.axis_size(axis)
    return lax.ppermute(cells, axis, [(i, i + 1) for i in range(count - 1)])


def from_next(cells, axis):
    count = lax.axis_size(axis)
    return lax.ppermute(cells, axis, [(i + 1, i) for i in range(count - 1)])


def exchange(cells):
    return (
        from_prev(cells, "tile"),
        from_next(cells, "tile"),
        from_prev(cells[:, -1:], "pair"),
        from_next(cells[:, :1], "pair"),
    )


def neighbours(cells, halo):
    above, below, left, right = halo
    west = jnp.concatenate([left, cells[:, :-1]], axis=1)
    east = jnp.concatenate([cells[:, 1:], right], axis=1)
    return above + below + west + east


def apply_operator(matrix, cells, halo):
    return jnp.dot(matrix, cells, precision=HIGHEST) - spatial_weight * neighbours(cells, halo)


def total(parts):
    count = lax.axis_size("pair") * lax.axis_size("tile")
    sent = jnp.broadcast_to(parts[None, :], (count, parts.shape[0]))
    got = lax.all_to_all(sent, ("pair", "tile"), 0, 0, tiled=True)
    return jnp.sum(got, axis=0)


def normal_matrix(weights):
    dates = jnp.arange(DATES, dtype=jnp.int32)
    offset = dates[None, :] - dates[:, None]
    upper = jnp.zeros((DATES, DATES), jnp.float32)
    for d in range(1, SPAN):
        upper = upper + jnp.where(offset == d, -weights[:, d : d + 1], 0.0)
    coupling = upper + upper.T
    degree = -jnp.sum(coupling, axis=1)
    diagonal = degree + (4.0 * spatial_weight + ridge_weight)
    return coupling + jnp.where(offset == 0, diagonal[:, None], 0.0) + temporal_weight * temporal_matrix()


def lane_value(vector, j):
    lanes = lax.broadcasted_iota(jnp.int32, vector.shape, 1)
    return jnp.sum(jnp.where(lanes == j, vector, 0.0), axis=1, keepdims=True)


def shifted(cells, left, right):
    width = cells.shape[1]
    lanes = lax.broadcasted_iota(jnp.int32, cells.shape, 1)
    probe = pltpu.roll(lanes, 1, 1)
    forward = probe == jnp.where(lanes == 0, width - 1, lanes - 1)
    one = pltpu.roll(cells, 1, 1)
    back = pltpu.roll(cells, width - 1, 1)
    west = jnp.where(lanes == 0, left, jnp.where(forward, one, back))
    east = jnp.where(lanes == width - 1, right, jnp.where(forward, back, one))
    return west, east


def operate(matrix, cells, above, below, left, right):
    west, east = shifted(cells, left, right)
    return jnp.dot(matrix, cells, precision=HIGHEST, preferred_element_type=jnp.float32) - spatial_weight * (
        above + below + west + east
    )


def send_buffer(send_ref, values):
    lanes = lax.broadcasted_iota(jnp.int32, (1, send_ref.shape[1]), 1)
    row = jnp.zeros((1, send_ref.shape[1]), jnp.float32)
    for j, value in enumerate(values):
        row = row + jnp.where(lanes == j, jnp.sum(value, keepdims=True), 0.0)
    send_ref[...] = jnp.broadcast_to(row, send_ref.shape)


def image_kernel(k_ref, v_ref, vu_ref, vd_ref, vl_ref, vr_ref, w_out):
    w_out[...] = operate(k_ref[...], v_ref[...], vu_ref[...], vd_ref[...], vl_ref[...], vr_ref[...])


def gram_kernel(k_ref, r_ref, w_ref, wu_ref, wd_ref, wl_ref, wr_ref, z_out, send_ref):
    r = r_ref[...]
    w = w_ref[...]
    z = operate(k_ref[...], w, wu_ref[...], wd_ref[...], wl_ref[...], wr_ref[...])
    z_out[...] = z
    send_buffer(send_ref, [r * r, r * w, w * w, r * z, w * z])


def krylov_kernel(k_ref, r_ref, w_ref, z_ref, zu_ref, zd_ref, zl_ref, zr_ref, y_out, send_ref):
    basis = [r_ref[...], w_ref[...], z_ref[...]]
    y = operate(k_ref[...], basis[2], zu_ref[...], zd_ref[...], zl_ref[...], zr_ref[...])
    y_out[...] = y
    basis.append(y)
    send_buffer(send_ref, [basis[i] * basis[j] for i, j in GRAM_PAIRS])


def combine_kernel(got_ref, r_ref, w_ref, z_ref, y_ref, x_out, res_out):
    sums = jnp.sum(got_ref[...], axis=0, keepdims=True)
    zero = jnp.zeros((1, 1), jnp.float32)
    gram = [[zero] * 4 for _ in range(4)]
    for n, (i, j) in enumerate(GRAM_PAIRS):
        gram[i][j] = gram[j][i] = lane_value(sums, n)

    def dot(u, v):
        total = zero
        for i in range(4):
            for j in range(4):
                if u[i] is not None and v[j] is not None:
                    total = total + u[i] * v[j] * gram[i][j]
        return total

    def mix(u, s, v):
        return [a if b is None else (s * b if a is None else a + s * b) for a, b in zip(u, v)]

    one = jnp.ones((1, 1), jnp.float32)
    residual = [one, None, None, None]
    direction = residual
    solution_field = [None] * 4
    norm_now = dot(residual, residual)
    for iteration in range(ITERS):
        image = [None] + direction[:3]
        alpha = norm_now / dot(direction, image)
        solution_field = mix(solution_field, alpha, direction)
        residual = mix(residual, -alpha, image)
        if iteration < ITERS - 1:
            norm_next = dot(residual, residual)
            direction = mix(residual, norm_next / norm_now, direction)
            norm_now = norm_next
    vectors = [r_ref, w_ref, z_ref, y_ref]
    x_out[...] = sum(c * v[...] for c, v in zip(solution_field, vectors) if c is not None)
    res_out[...] = sum(c * v[...] for c, v in zip(residual, vectors) if c is not None)


def step_scalars(got_ref, scal_ref):
    sums = jnp.sum(got_ref[...], axis=0, keepdims=True)
    previous = scal_ref[...]
    norm = lane_value(sums, 0)
    beta = norm / lane_value(previous, 0)
    curvature = lane_value(sums, 1) + beta * (lane_value(sums, 2) + lane_value(sums, 3)) + beta * beta * lane_value(sums, 4)
    return norm, beta, norm / curvature


def last_kernel(got_ref, scal_ref, r_ref, p_ref, q_ref, x_ref, w_ref, x_out, r_out):
    norm, beta, alpha = step_scalars(got_ref, scal_ref)
    p = r_ref[...] + beta * p_ref[...]
    q = w_ref[...] + beta * q_ref[...]
    x_out[...] = x_ref[...] + alpha * p
    r_out[...] = r_ref[...] - alpha * q


def call(kernel, shapes, *args):
    resident = pl.BlockSpec(memory_space=pltpu.VMEM)
    return pl.pallas_call(
        kernel,
        out_shape=[jax.ShapeDtypeStruct(s, jnp.float32) for s in shapes],
        in_specs=[resident] * len(args),
        out_specs=[resident] * len(shapes),
    )(*args)


def reduce_all(send):
    return lax.all_to_all(send, ("pair", "tile"), 0, 0, tiled=True)


def exchange_rows_cols(cells):
    return (
        from_prev(cells, "tile"),
        from_next(cells, "tile"),
        from_prev(cells[:, -1:], "pair"),
        from_next(cells[:, :1], "pair"),
    )


def body(phase, incidence, pair_weight):
    groups = lax.axis_size("pair")
    cols = phase.shape[2] // groups
    padded = jnp.pad(phase[:, 0, :], ((0, 0), (1, 1)))
    windows = jnp.stack([padded[:, j * cols : j * cols + cols + 2] for j in range(groups)])
    meta = jnp.stack(
        [incidence[:, 0].astype(jnp.float32), incidence[:, 1].astype(jnp.float32), pair_weight], axis=1
    )
    meta = jnp.pad(meta, ((0, 0), (0, 3)))
    chunks = jnp.concatenate([windows, jnp.broadcast_to(meta, (groups,) + meta.shape)], axis=2)
    got = lax.all_to_all(chunks, "pair", 0, 0, tiled=True).reshape(-1, chunks.shape[2])
    values = got[:, : cols + 2]
    earlier = got[:, cols + 2 : cols + 3]
    later = got[:, cols + 3 : cols + 4]
    weight = got[:, cols + 4 : cols + 5]
    dates = jnp.arange(DATES, dtype=jnp.float32)
    network = ((dates[None, :] == later).astype(jnp.float32) - (dates[None, :] == earlier).astype(jnp.float32)).astype(
        jnp.bfloat16
    )
    weighted = weight * values
    high = lax.reduce_precision(weighted, exponent_bits=8, mantissa_bits=7)
    rest = weighted - high
    middle = lax.reduce_precision(rest, exponent_bits=8, mantissa_bits=7)
    low = rest - middle
    high, middle, low = (part.astype(jnp.bfloat16) for part in (high, middle, low))
    width = values.shape[1]
    pieces = jnp.einsum(
        "kt,kc->tc", network, jnp.concatenate([high, middle, low], axis=1), preferred_element_type=jnp.float32
    )
    right_wide = pieces[:, :width] + pieces[:, width : 2 * width] + pieces[:, 2 * width :]
    span_hot = (jnp.arange(SPAN, dtype=jnp.float32)[None, :] == (later - earlier)).astype(jnp.float32)
    start_hot = (dates[None, :] == earlier).astype(jnp.float32)
    span_weights = jnp.einsum("kt,kd->td", start_hot, span_hot * weight, precision=HIGHEST)
    matrix = normal_matrix(span_weights)
    residual = right_wide[:, 1:-1]
    residual_halo = (
        from_prev(residual, "tile"),
        from_next(residual, "tile"),
        right_wide[:, :1],
        right_wide[:, -1:],
    )
    count = lax.axis_size("pair") * lax.axis_size("tile")
    field = residual.shape
    lanes = 128
    send_shape = (count, lanes)
    (w0,) = call(image_kernel, [field], matrix, residual, *residual_halo)
    w0_halo = exchange_rows_cols(w0)
    (z0,) = call(image_kernel, [field], matrix, w0, *w0_halo)
    z0_halo = exchange_rows_cols(z0)
    y0, send = call(krylov_kernel, [field, send_shape], matrix, residual, w0, z0, *z0_halo)
    got = reduce_all(send)
    solution_field, residual = call(combine_kernel, [field, field], got, residual, w0, z0, y0)
    return (solution_field[:, None, :], residual[:, None, :])


def solution(mesh):
    return jax.shard_map(
        body,
        mesh=mesh,
        in_specs=(P("pair", "tile", None), P("pair", None), P("pair")),
        out_specs=(P(None, "tile", "pair"), P(None, "tile", "pair")),
        check_vma=False,
    )
```

```python
import functools

import numpy as np
import jax
import jax.numpy as jnp
from jax import lax
from jax.sharding import PartitionSpec as P
from jax.experimental import pallas as pl
from jax.experimental.pallas import tpu as pltpu

DATES = 400
ITERS = 3
SPAN = 8
GRAM_PAIRS = ((0, 0), (0, 1), (0, 2), (0, 3), (1, 1), (1, 2), (1, 3), (2, 2), (2, 3))

temporal_weight = 2.0
spatial_weight = 0.5
ridge_weight = 0.05

HIGHEST = lax.Precision.HIGHEST


def temporal_matrix():
    second = np.zeros((DATES - 2, DATES), np.float64)
    rows = np.arange(DATES - 2)
    second[rows, rows] = 1.0
    second[rows, rows + 1] = -2.0
    second[rows, rows + 2] = 1.0
    return (second.T @ second).astype(np.float32)


def from_prev(cells, axis):
    count = lax.axis_size(axis)
    return lax.ppermute(cells, axis, [(i, i + 1) for i in range(count - 1)])


def from_next(cells, axis):
    count = lax.axis_size(axis)
    return lax.ppermute(cells, axis, [(i + 1, i) for i in range(count - 1)])


def exchange(cells):
    return (
        from_prev(cells, "tile"),
        from_next(cells, "tile"),
        from_prev(cells[:, -1:], "pair"),
        from_next(cells[:, :1], "pair"),
    )


def neighbours(cells, halo):
    above, below, left, right = halo
    west = jnp.concatenate([left, cells[:, :-1]], axis=1)
    east = jnp.concatenate([cells[:, 1:], right], axis=1)
    return above + below + west + east


def apply_operator(matrix, cells, halo):
    return jnp.dot(matrix, cells, precision=HIGHEST) - spatial_weight * neighbours(cells, halo)


def total(parts):
    count = lax.axis_size("pair") * lax.axis_size("tile")
    sent = jnp.broadcast_to(parts[None, :], (count, parts.shape[0]))
    got = lax.all_to_all(sent, ("pair", "tile"), 0, 0, tiled=True)
    return jnp.sum(got, axis=0)


def normal_matrix(weights):
    dates = jnp.arange(DATES, dtype=jnp.int32)
    offset = dates[None, :] - dates[:, None]
    upper = jnp.zeros((DATES, DATES), jnp.float32)
    for d in range(1, SPAN):
        upper = upper + jnp.where(offset == d, -weights[:, d : d + 1], 0.0)
    coupling = upper + upper.T
    degree = -jnp.sum(coupling, axis=1)
    diagonal = degree + (4.0 * spatial_weight + ridge_weight)
    return coupling + jnp.where(offset == 0, diagonal[:, None], 0.0) + temporal_weight * temporal_matrix()


def lane_value(vector, j):
    lanes = lax.broadcasted_iota(jnp.int32, vector.shape, 1)
    return jnp.sum(jnp.where(lanes == j, vector, 0.0), axis=1, keepdims=True)


def shifted(cells, left, right):
    width = cells.shape[1]
    lanes = lax.broadcasted_iota(jnp.int32, cells.shape, 1)
    probe = pltpu.roll(lanes, 1, 1)
    forward = probe == jnp.where(lanes == 0, width - 1, lanes - 1)
    one = pltpu.roll(cells, 1, 1)
    back = pltpu.roll(cells, width - 1, 1)
    west = jnp.where(lanes == 0, left, jnp.where(forward, one, back))
    east = jnp.where(lanes == width - 1, right, jnp.where(forward, back, one))
    return west, east


def operate(matrix, cells, above, below, left, right):
    west, east = shifted(cells, left, right)
    return jnp.dot(matrix, cells, precision=HIGHEST, preferred_element_type=jnp.float32) - spatial_weight * (
        above + below + west + east
    )


def send_buffer(send_ref, values):
    lanes = lax.broadcasted_iota(jnp.int32, (1, send_ref.shape[1]), 1)
    row = jnp.zeros((1, send_ref.shape[1]), jnp.float32)
    for j, value in enumerate(values):
        row = row + jnp.where(lanes == j, jnp.sum(value, keepdims=True), 0.0)
    send_ref[...] = jnp.broadcast_to(row, send_ref.shape)


def image_kernel(index, shift_ref, k_ref, v_ref, vu_ref, vd_ref, vl_ref, vr_ref, w_out):
    v = v_ref[...]
    w_out[...] = operate(k_ref[...], v, vu_ref[...], vd_ref[...], vl_ref[...], vr_ref[...]) - lane_value(
        shift_ref[...], index
    ) * v


def gram_kernel(k_ref, r_ref, w_ref, wu_ref, wd_ref, wl_ref, wr_ref, z_out, send_ref):
    r = r_ref[...]
    w = w_ref[...]
    z = operate(k_ref[...], w, wu_ref[...], wd_ref[...], wl_ref[...], wr_ref[...])
    z_out[...] = z
    send_buffer(send_ref, [r * r, r * w, w * w, r * z, w * z])


def krylov_kernel(shift_ref, k_ref, r_ref, w_ref, z_ref, zu_ref, zd_ref, zl_ref, zr_ref, y_out, send_ref):
    basis = [r_ref[...], w_ref[...], z_ref[...]]
    y = operate(k_ref[...], basis[2], zu_ref[...], zd_ref[...], zl_ref[...], zr_ref[...]) - lane_value(
        shift_ref[...], 2
    ) * basis[2]
    y_out[...] = y
    basis.append(y)
    send_buffer(send_ref, [basis[i] * basis[j] for i, j in GRAM_PAIRS])


def combine_kernel(shift_ref, got_ref, r_ref, w_ref, z_ref, y_ref, x_out, res_out):
    sums = jnp.sum(got_ref[...], axis=0, keepdims=True)
    shifts = [lane_value(shift_ref[...], k) for k in range(3)]
    zero = jnp.zeros((1, 1), jnp.float32)
    gram = [[zero] * 4 for _ in range(4)]
    for n, (i, j) in enumerate(GRAM_PAIRS):
        gram[i][j] = gram[j][i] = lane_value(sums, n)

    def dot(u, v):
        total = zero
        for i in range(4):
            for j in range(4):
                if u[i] is not None and v[j] is not None:
                    total = total + u[i] * v[j] * gram[i][j]
        return total

    def mix(u, s, v):
        return [a if b is None else (s * b if a is None else a + s * b) for a, b in zip(u, v)]

    one = jnp.ones((1, 1), jnp.float32)
    residual = [one, None, None, None]
    direction = residual
    solution_field = [None] * 4
    norm_now = dot(residual, residual)
    for iteration in range(ITERS):
        image = [None] * 4
        for k in range(3):
            if direction[k] is not None:
                image = mix(image, shifts[k], [None] * k + [direction[k]] + [None] * (3 - k))
                image = mix(image, one, [None] * (k + 1) + [direction[k]] + [None] * (2 - k))
        alpha = norm_now / dot(direction, image)
        solution_field = mix(solution_field, alpha, direction)
        residual = mix(residual, -alpha, image)
        if iteration < ITERS - 1:
            norm_next = dot(residual, residual)
            direction = mix(residual, norm_next / norm_now, direction)
            norm_now = norm_next
    vectors = [r_ref, w_ref, z_ref, y_ref]
    x_out[...] = sum(c * v[...] for c, v in zip(solution_field, vectors) if c is not None)
    res_out[...] = sum(c * v[...] for c, v in zip(residual, vectors) if c is not None)


def step_scalars(got_ref, scal_ref):
    sums = jnp.sum(got_ref[...], axis=0, keepdims=True)
    previous = scal_ref[...]
    norm = lane_value(sums, 0)
    beta = norm / lane_value(previous, 0)
    curvature = lane_value(sums, 1) + beta * (lane_value(sums, 2) + lane_value(sums, 3)) + beta * beta * lane_value(sums, 4)
    return norm, beta, norm / curvature


def last_kernel(got_ref, scal_ref, r_ref, p_ref, q_ref, x_ref, w_ref, x_out, r_out):
    norm, beta, alpha = step_scalars(got_ref, scal_ref)
    p = r_ref[...] + beta * p_ref[...]
    q = w_ref[...] + beta * q_ref[...]
    x_out[...] = x_ref[...] + alpha * p
    r_out[...] = r_ref[...] - alpha * q


def call(kernel, shapes, *args):
    resident = pl.BlockSpec(memory_space=pltpu.VMEM)
    return pl.pallas_call(
        kernel,
        out_shape=[jax.ShapeDtypeStruct(s, jnp.float32) for s in shapes],
        in_specs=[resident] * len(args),
        out_specs=[resident] * len(shapes),
    )(*args)


def reduce_all(send):
    return lax.all_to_all(send, ("pair", "tile"), 0, 0, tiled=True)


def exchange_rows_cols(cells):
    return (
        from_prev(cells, "tile"),
        from_next(cells, "tile"),
        from_prev(cells[:, -1:], "pair"),
        from_next(cells[:, :1], "pair"),
    )


def body(phase, incidence, pair_weight):
    groups = lax.axis_size("pair")
    cols = phase.shape[2] // groups
    padded = jnp.pad(phase[:, 0, :], ((0, 0), (1, 1)))
    windows = jnp.stack([padded[:, j * cols : j * cols + cols + 2] for j in range(groups)])
    meta = jnp.stack(
        [incidence[:, 0].astype(jnp.float32), incidence[:, 1].astype(jnp.float32), pair_weight], axis=1
    )
    meta = jnp.pad(meta, ((0, 0), (0, 3)))
    chunks = jnp.concatenate([windows, jnp.broadcast_to(meta, (groups,) + meta.shape)], axis=2)
    got = lax.all_to_all(chunks, "pair", 0, 0, tiled=True).reshape(-1, chunks.shape[2])
    values = got[:, : cols + 2]
    earlier = got[:, cols + 2 : cols + 3]
    later = got[:, cols + 3 : cols + 4]
    weight = got[:, cols + 4 : cols + 5]
    dates = jnp.arange(DATES, dtype=jnp.float32)
    network = ((dates[None, :] == later).astype(jnp.float32) - (dates[None, :] == earlier).astype(jnp.float32)).astype(
        jnp.bfloat16
    )
    weighted = weight * values
    high = lax.reduce_precision(weighted, exponent_bits=8, mantissa_bits=7)
    rest = weighted - high
    middle = lax.reduce_precision(rest, exponent_bits=8, mantissa_bits=7)
    low = rest - middle
    high, middle, low = (part.astype(jnp.bfloat16) for part in (high, middle, low))
    width = values.shape[1]
    pieces = jnp.einsum(
        "kt,kc->tc", network, jnp.concatenate([high, middle, low], axis=1), preferred_element_type=jnp.float32
    )
    right_wide = pieces[:, :width] + pieces[:, width : 2 * width] + pieces[:, 2 * width :]
    span_hot = (jnp.arange(SPAN, dtype=jnp.float32)[None, :] == (later - earlier)).astype(jnp.float32)
    start_hot = (dates[None, :] == earlier).astype(jnp.float32)
    span_weights = jnp.einsum("kt,kd->td", start_hot, span_hot * weight, precision=HIGHEST)
    matrix = normal_matrix(span_weights)
    residual = right_wide[:, 1:-1]
    residual_halo = (
        from_prev(residual, "tile"),
        from_next(residual, "tile"),
        right_wide[:, :1],
        right_wide[:, -1:],
    )
    count = lax.axis_size("pair") * lax.axis_size("tile")
    field = residual.shape
    lanes = 128
    send_shape = (count, lanes)
    bound = jnp.max(jnp.sum(jnp.abs(matrix), axis=1)) + 4.0 * spatial_weight
    nodes = np.cos(np.array([1.0, 5.0, 3.0]) * np.pi / 6.0).astype(np.float32)
    shift = jnp.zeros((1, lanes), jnp.float32).at[0, :3].set(0.5 * bound * (1.0 + nodes))
    (w0,) = call(functools.partial(image_kernel, 0), [field], shift, matrix, residual, *residual_halo)
    w0_halo = exchange_rows_cols(w0)
    (z0,) = call(functools.partial(image_kernel, 1), [field], shift, matrix, w0, *w0_halo)
    z0_halo = exchange_rows_cols(z0)
    y0, send = call(krylov_kernel, [field, send_shape], shift, matrix, residual, w0, z0, *z0_halo)
    got = reduce_all(send)
    solution_field, residual = call(combine_kernel, [field, field], shift, got, residual, w0, z0, y0)
    return (solution_field[:, None, :], residual[:, None, :])


def solution(mesh):
    return jax.shard_map(
        body,
        mesh=mesh,
        in_specs=(P("pair", "tile", None), P("pair", None), P("pair")),
        out_specs=(P(None, "tile", "pair"), P(None, "tile", "pair")),
        check_vma=False,
    )
```

```python
import numpy as np
import jax
import jax.numpy as jnp
from jax import lax
from jax.sharding import PartitionSpec as P
from jax.experimental import pallas as pl
from jax.experimental.pallas import tpu as pltpu

DATES = 400
ITERS = 3
SPAN = 8

temporal_weight = 2.0
spatial_weight = 0.5
ridge_weight = 0.05

HIGHEST = lax.Precision.HIGHEST


def temporal_matrix():
    second = np.zeros((DATES - 2, DATES), np.float64)
    rows = np.arange(DATES - 2)
    second[rows, rows] = 1.0
    second[rows, rows + 1] = -2.0
    second[rows, rows + 2] = 1.0
    return (second.T @ second).astype(np.float32)


def from_prev(cells, axis):
    count = lax.axis_size(axis)
    return lax.ppermute(cells, axis, [(i, i + 1) for i in range(count - 1)])


def from_next(cells, axis):
    count = lax.axis_size(axis)
    return lax.ppermute(cells, axis, [(i + 1, i) for i in range(count - 1)])


def exchange(cells):
    return (
        from_prev(cells, "tile"),
        from_next(cells, "tile"),
        from_prev(cells[:, -1:], "pair"),
        from_next(cells[:, :1], "pair"),
    )


def neighbours(cells, halo):
    above, below, left, right = halo
    west = jnp.concatenate([left, cells[:, :-1]], axis=1)
    east = jnp.concatenate([cells[:, 1:], right], axis=1)
    return above + below + west + east


def apply_operator(matrix, cells, halo):
    return jnp.dot(matrix, cells, precision=HIGHEST) - spatial_weight * neighbours(cells, halo)


def total(parts):
    count = lax.axis_size("pair") * lax.axis_size("tile")
    sent = jnp.broadcast_to(parts[None, :], (count, parts.shape[0]))
    got = lax.all_to_all(sent, ("pair", "tile"), 0, 0, tiled=True)
    return jnp.sum(got, axis=0)


def normal_matrix(weights):
    dates = jnp.arange(DATES, dtype=jnp.int32)
    offset = dates[None, :] - dates[:, None]
    upper = jnp.zeros((DATES, DATES), jnp.float32)
    for d in range(1, SPAN):
        upper = upper + jnp.where(offset == d, -weights[:, d : d + 1], 0.0)
    coupling = upper + upper.T
    degree = -jnp.sum(coupling, axis=1)
    diagonal = degree + (4.0 * spatial_weight + ridge_weight)
    return coupling + jnp.where(offset == 0, diagonal[:, None], 0.0) + temporal_weight * temporal_matrix()


def lane_value(vector, j):
    lanes = lax.broadcasted_iota(jnp.int32, vector.shape, 1)
    return jnp.sum(jnp.where(lanes == j, vector, 0.0), axis=1, keepdims=True)


def shifted(cells, left, right):
    width = cells.shape[1]
    lanes = lax.broadcasted_iota(jnp.int32, cells.shape, 1)
    probe = pltpu.roll(lanes, 1, 1)
    forward = probe == jnp.where(lanes == 0, width - 1, lanes - 1)
    one = pltpu.roll(cells, 1, 1)
    back = pltpu.roll(cells, width - 1, 1)
    west = jnp.where(lanes == 0, left, jnp.where(forward, one, back))
    east = jnp.where(lanes == width - 1, right, jnp.where(forward, back, one))
    return west, east


def operate(matrix, cells, above, below, left, right):
    west, east = shifted(cells, left, right)
    return jnp.dot(matrix, cells, precision=HIGHEST, preferred_element_type=jnp.float32) - spatial_weight * (
        above + below + west + east
    )


def send_buffer(send_ref, values):
    lanes = lax.broadcasted_iota(jnp.int32, (1, send_ref.shape[1]), 1)
    row = jnp.zeros((1, send_ref.shape[1]), jnp.float32)
    for j, value in enumerate(values):
        row = row + jnp.where(lanes == j, jnp.sum(value, keepdims=True), 0.0)
    send_ref[...] = jnp.broadcast_to(row, send_ref.shape)


def image_kernel(k_ref, v_ref, vu_ref, vd_ref, vl_ref, vr_ref, w_out):
    w_out[...] = operate(k_ref[...], v_ref[...], vu_ref[...], vd_ref[...], vl_ref[...], vr_ref[...])


def gram_kernel(k_ref, r_ref, w_ref, wu_ref, wd_ref, wl_ref, wr_ref, z_out, send_ref):
    r = r_ref[...]
    w = w_ref[...]
    z = operate(k_ref[...], w, wu_ref[...], wd_ref[...], wl_ref[...], wr_ref[...])
    z_out[...] = z
    send_buffer(send_ref, [r * r, r * w, w * w, r * z, w * z])


def block_kernel(got_ref, k_ref, r_ref, w_ref, z_ref, ru_ref, rd_ref, rl_ref, rr_ref, wu_ref, wd_ref, wl_ref, wr_ref,
                 zu_ref, zd_ref, zl_ref, zr_ref, r_out, p_out, q_out, x_out, w_out, send_ref, scal_out):
    sums = jnp.sum(got_ref[...], axis=0, keepdims=True)
    norm_first = lane_value(sums, 0)
    curvature_first = lane_value(sums, 1)
    alpha_first = norm_first / curvature_first
    norm = norm_first - 2.0 * alpha_first * curvature_first + alpha_first * alpha_first * lane_value(sums, 2)
    beta = norm / norm_first
    a = 1.0 + beta
    b = -alpha_first
    curvature = a * a * curvature_first + a * b * (lane_value(sums, 3) + lane_value(sums, 2)) + b * b * lane_value(sums, 4)
    alpha = norm / curvature
    r0 = r_ref[...]
    w0 = w_ref[...]
    z0 = z_ref[...]
    p = a * r0 + b * w0
    q = a * w0 + b * z0
    p_out[...] = p
    q_out[...] = q
    x_out[...] = alpha_first * r0 + alpha * p
    r = (r0 - alpha_first * w0) - alpha * q
    r_out[...] = r
    halo = []
    for hr, hw, hz in zip((ru_ref, rd_ref, rl_ref, rr_ref), (wu_ref, wd_ref, wl_ref, wr_ref), (zu_ref, zd_ref, zl_ref, zr_ref)):
        halo.append((hr[...] - alpha_first * hw[...]) - alpha * (a * hw[...] + b * hz[...]))
    w = operate(k_ref[...], r, *halo)
    w_out[...] = w
    send_buffer(send_ref, [r * r, r * w, r * q, p * w, p * q])
    lanes = lax.broadcasted_iota(jnp.int32, scal_out.shape, 1)
    scal_out[...] = jnp.where(lanes == 0, norm, 0.0)


def step_scalars(got_ref, scal_ref):
    sums = jnp.sum(got_ref[...], axis=0, keepdims=True)
    previous = scal_ref[...]
    norm = lane_value(sums, 0)
    beta = norm / lane_value(previous, 0)
    curvature = lane_value(sums, 1) + beta * (lane_value(sums, 2) + lane_value(sums, 3)) + beta * beta * lane_value(sums, 4)
    return norm, beta, norm / curvature


def last_kernel(got_ref, scal_ref, r_ref, p_ref, q_ref, x_ref, w_ref, x_out, r_out):
    norm, beta, alpha = step_scalars(got_ref, scal_ref)
    p = r_ref[...] + beta * p_ref[...]
    q = w_ref[...] + beta * q_ref[...]
    x_out[...] = x_ref[...] + alpha * p
    r_out[...] = r_ref[...] - alpha * q


def call(kernel, shapes, *args):
    resident = pl.BlockSpec(memory_space=pltpu.VMEM)
    return pl.pallas_call(
        kernel,
        out_shape=[jax.ShapeDtypeStruct(s, jnp.float32) for s in shapes],
        in_specs=[resident] * len(args),
        out_specs=[resident] * len(shapes),
    )(*args)


def reduce_all(send):
    return lax.all_to_all(send, ("pair", "tile"), 0, 0, tiled=True)


def exchange_rows_cols(cells):
    return (
        from_prev(cells, "tile"),
        from_next(cells, "tile"),
        from_prev(cells[:, -1:], "pair"),
        from_next(cells[:, :1], "pair"),
    )


def body(phase, incidence, pair_weight):
    groups = lax.axis_size("pair")
    cols = phase.shape[2] // groups
    padded = jnp.pad(phase[:, 0, :], ((0, 0), (2, 2)))
    windows = jnp.stack([padded[:, j * cols : j * cols + cols + 4] for j in range(groups)])
    meta = jnp.stack(
        [incidence[:, 0].astype(jnp.float32), incidence[:, 1].astype(jnp.float32), pair_weight], axis=1
    )
    meta = jnp.pad(meta, ((0, 0), (0, 1)))
    chunks = jnp.concatenate([windows, jnp.broadcast_to(meta, (groups,) + meta.shape)], axis=2)
    got = lax.all_to_all(chunks, "pair", 0, 0, tiled=True).reshape(-1, chunks.shape[2])
    values = got[:, : cols + 4]
    earlier = got[:, cols + 4 : cols + 5]
    later = got[:, cols + 5 : cols + 6]
    weight = got[:, cols + 6 : cols + 7]
    dates = jnp.arange(DATES, dtype=jnp.float32)
    network = ((dates[None, :] == later).astype(jnp.float32) - (dates[None, :] == earlier).astype(jnp.float32)).astype(
        jnp.bfloat16
    )
    weighted = weight * values
    high = lax.reduce_precision(weighted, exponent_bits=8, mantissa_bits=7)
    rest = weighted - high
    middle = lax.reduce_precision(rest, exponent_bits=8, mantissa_bits=7)
    low = rest - middle
    high, middle, low = (part.astype(jnp.bfloat16) for part in (high, middle, low))
    width = values.shape[1]
    pieces = jnp.einsum(
        "kt,kc->tc", network, jnp.concatenate([high, middle, low], axis=1), preferred_element_type=jnp.float32
    )
    right_wide = pieces[:, :width] + pieces[:, width : 2 * width] + pieces[:, 2 * width :]
    span_hot = (jnp.arange(SPAN, dtype=jnp.float32)[None, :] == (later - earlier)).astype(jnp.float32)
    start_hot = (dates[None, :] == earlier).astype(jnp.float32)
    span_weights = jnp.einsum("kt,kd->td", start_hot, span_hot * weight, precision=HIGHEST)
    matrix = normal_matrix(span_weights)
    residual = right_wide[:, 2:-2]
    outer = jnp.concatenate([right_wide[:, 1], right_wide[:, -2], jnp.zeros((8 * 128 - 2 * DATES,), jnp.float32)])
    payload = jnp.concatenate([residual, outer.reshape(8, 128)], axis=0)
    above_wide = from_prev(payload, "tile")
    below_wide = from_next(payload, "tile")
    residual_halo = (above_wide[:DATES], below_wide[:DATES], right_wide[:, 1:2], right_wide[:, -2:-1])
    above_outer = above_wide[DATES:].reshape(-1)
    below_outer = below_wide[DATES:].reshape(-1)
    edge = jnp.stack([right_wide[:, 1], right_wide[:, -2]], axis=1)
    edge_rows = jnp.stack([above_outer[:DATES] + below_outer[:DATES], above_outer[DATES : 2 * DATES] + below_outer[DATES : 2 * DATES]], axis=1)
    edge_cols = jnp.stack([right_wide[:, 0] + right_wide[:, 2], right_wide[:, -3] + right_wide[:, -1]], axis=1)
    edge_image = jnp.dot(matrix, edge, precision=HIGHEST) - spatial_weight * (edge_rows + edge_cols)
    place = lax.axis_index("pair")
    inside = jnp.stack([place > 0, place < groups - 1]).astype(jnp.float32)
    edge_image = edge_image * inside[None, :]
    count = lax.axis_size("pair") * lax.axis_size("tile")
    field = residual.shape
    lanes = 128
    send_shape = (count, lanes)
    (w0,) = call(image_kernel, [field], matrix, residual, *residual_halo)
    w0_halo = (from_prev(w0, "tile"), from_next(w0, "tile"), edge_image[:, 0:1], edge_image[:, 1:2])
    z0, send = call(gram_kernel, [field, send_shape], matrix, residual, w0, *w0_halo)
    got = reduce_all(send)
    z0_halo = exchange_rows_cols(z0)
    r2, p1, q1, x2, w2, send, scal = call(
        block_kernel,
        [field, field, field, field, field, send_shape, (1, lanes)],
        got, matrix, residual, w0, z0, *residual_halo, *w0_halo, *z0_halo,
    )
    got = reduce_all(send)
    solution_field, residual = call(last_kernel, [field, field], got, scal, r2, p1, q1, x2, w2)
    return (solution_field[:, None, :], residual[:, None, :])


def solution(mesh):
    return jax.shard_map(
        body,
        mesh=mesh,
        in_specs=(P("pair", "tile", None), P("pair", None), P("pair")),
        out_specs=(P(None, "tile", "pair"), P(None, "tile", "pair")),
        check_vma=False,
    )
```

```python
import numpy as np
import jax
import jax.numpy as jnp
from jax import lax
from jax.sharding import PartitionSpec as P
from jax.experimental import pallas as pl
from jax.experimental.pallas import tpu as pltpu

DATES = 400
ITERS = 3
SPAN = 8

temporal_weight = 2.0
spatial_weight = 0.5
ridge_weight = 0.05

HIGHEST = lax.Precision.HIGHEST


def temporal_matrix():
    second = np.zeros((DATES - 2, DATES), np.float64)
    rows = np.arange(DATES - 2)
    second[rows, rows] = 1.0
    second[rows, rows + 1] = -2.0
    second[rows, rows + 2] = 1.0
    return (second.T @ second).astype(np.float32)


def from_prev(cells, axis):
    count = lax.axis_size(axis)
    return lax.ppermute(cells, axis, [(i, i + 1) for i in range(count - 1)])


def from_next(cells, axis):
    count = lax.axis_size(axis)
    return lax.ppermute(cells, axis, [(i + 1, i) for i in range(count - 1)])


def exchange(cells):
    return (
        from_prev(cells, "tile"),
        from_next(cells, "tile"),
        from_prev(cells[:, -1:], "pair"),
        from_next(cells[:, :1], "pair"),
    )


def neighbours(cells, halo):
    above, below, left, right = halo
    west = jnp.concatenate([left, cells[:, :-1]], axis=1)
    east = jnp.concatenate([cells[:, 1:], right], axis=1)
    return above + below + west + east


def apply_operator(matrix, cells, halo):
    return jnp.dot(matrix, cells, precision=HIGHEST) - spatial_weight * neighbours(cells, halo)


def total(parts):
    count = lax.axis_size("pair") * lax.axis_size("tile")
    sent = jnp.broadcast_to(parts[None, :], (count, parts.shape[0]))
    got = lax.all_to_all(sent, ("pair", "tile"), 0, 0, tiled=True)
    return jnp.sum(got, axis=0)


def normal_matrix(weights):
    dates = jnp.arange(DATES, dtype=jnp.int32)
    offset = dates[None, :] - dates[:, None]
    upper = jnp.zeros((DATES, DATES), jnp.float32)
    for d in range(1, SPAN):
        upper = upper + jnp.where(offset == d, -weights[:, d : d + 1], 0.0)
    coupling = upper + upper.T
    degree = -jnp.sum(coupling, axis=1)
    diagonal = degree + (4.0 * spatial_weight + ridge_weight)
    return coupling + jnp.where(offset == 0, diagonal[:, None], 0.0) + temporal_weight * temporal_matrix()


def lane_value(vector, j):
    lanes = lax.broadcasted_iota(jnp.int32, vector.shape, 1)
    return jnp.sum(jnp.where(lanes == j, vector, 0.0), axis=1, keepdims=True)


def shifted(cells, left, right):
    width = cells.shape[1]
    lanes = lax.broadcasted_iota(jnp.int32, cells.shape, 1)
    probe = pltpu.roll(lanes, 1, 1)
    forward = probe == jnp.where(lanes == 0, width - 1, lanes - 1)
    one = pltpu.roll(cells, 1, 1)
    back = pltpu.roll(cells, width - 1, 1)
    west = jnp.where(lanes == 0, left, jnp.where(forward, one, back))
    east = jnp.where(lanes == width - 1, right, jnp.where(forward, back, one))
    return west, east


def operate(matrix, cells, above, below, left, right):
    west, east = shifted(cells, left, right)
    return jnp.dot(matrix, cells, precision=HIGHEST, preferred_element_type=jnp.float32) - spatial_weight * (
        above + below + west + east
    )


def send_buffer(send_ref, values):
    lanes = lax.broadcasted_iota(jnp.int32, (1, send_ref.shape[1]), 1)
    row = jnp.zeros((1, send_ref.shape[1]), jnp.float32)
    for j, value in enumerate(values):
        row = row + jnp.where(lanes == j, jnp.sum(value, keepdims=True), 0.0)
    send_ref[...] = jnp.broadcast_to(row, send_ref.shape)


def head(ref):
    return ref[0:DATES]


def image_kernel(k_ref, v_ref, vu_ref, vd_ref, vl_ref, vr_ref, w_out):
    w_out[...] = operate(k_ref[...], v_ref[...], head(vu_ref), head(vd_ref), vl_ref[...], vr_ref[...])


def gram_kernel(k_ref, r_ref, w_ref, wu_ref, wd_ref, wl_ref, wr_ref, z_out, send_ref):
    r = r_ref[...]
    w = w_ref[...]
    z = operate(k_ref[...], w, wu_ref[...], wd_ref[...], wl_ref[...], wr_ref[...])
    z_out[...] = z
    send_buffer(send_ref, [r * r, r * w, w * w, r * z, w * z])


def block_kernel(got_ref, k_ref, r_ref, w_ref, z_ref, ru_ref, rd_ref, rl_ref, rr_ref, wu_ref, wd_ref, wl_ref, wr_ref,
                 zu_ref, zd_ref, zl_ref, zr_ref, r_out, p_out, q_out, x_out, w_out, send_ref, scal_out):
    sums = jnp.sum(got_ref[...], axis=0, keepdims=True)
    norm_first = lane_value(sums, 0)
    curvature_first = lane_value(sums, 1)
    alpha_first = norm_first / curvature_first
    norm = norm_first - 2.0 * alpha_first * curvature_first + alpha_first * alpha_first * lane_value(sums, 2)
    beta = norm / norm_first
    a = 1.0 + beta
    b = -alpha_first
    curvature = a * a * curvature_first + a * b * (lane_value(sums, 3) + lane_value(sums, 2)) + b * b * lane_value(sums, 4)
    alpha = norm / curvature
    r0 = r_ref[...]
    w0 = w_ref[...]
    z0 = z_ref[...]
    p = a * r0 + b * w0
    q = a * w0 + b * z0
    p_out[...] = p
    q_out[...] = q
    x_out[...] = alpha_first * r0 + alpha * p
    r = (r0 - alpha_first * w0) - alpha * q
    r_out[...] = r
    halo = []
    for hr, hw, hz in zip((ru_ref, rd_ref, rl_ref, rr_ref), (wu_ref, wd_ref, wl_ref, wr_ref), (zu_ref, zd_ref, zl_ref, zr_ref)):
        halo.append((head(hr) - alpha_first * hw[...]) - alpha * (a * hw[...] + b * hz[...]))
    w = operate(k_ref[...], r, *halo)
    w_out[...] = w
    send_buffer(send_ref, [r * r, r * w, r * q, p * w, p * q])
    lanes = lax.broadcasted_iota(jnp.int32, scal_out.shape, 1)
    scal_out[...] = jnp.where(lanes == 0, norm, 0.0)


def step_scalars(got_ref, scal_ref):
    sums = jnp.sum(got_ref[...], axis=0, keepdims=True)
    previous = scal_ref[...]
    norm = lane_value(sums, 0)
    beta = norm / lane_value(previous, 0)
    curvature = lane_value(sums, 1) + beta * (lane_value(sums, 2) + lane_value(sums, 3)) + beta * beta * lane_value(sums, 4)
    return norm, beta, norm / curvature


def last_kernel(got_ref, scal_ref, r_ref, p_ref, q_ref, x_ref, w_ref, x_out, r_out):
    norm, beta, alpha = step_scalars(got_ref, scal_ref)
    p = r_ref[...] + beta * p_ref[...]
    q = w_ref[...] + beta * q_ref[...]
    x_out[...] = x_ref[...] + alpha * p
    r_out[...] = r_ref[...] - alpha * q


def call(kernel, shapes, *args):
    resident = pl.BlockSpec(memory_space=pltpu.VMEM)
    return pl.pallas_call(
        kernel,
        out_shape=[jax.ShapeDtypeStruct(s, jnp.float32) for s in shapes],
        in_specs=[resident] * len(args),
        out_specs=[resident] * len(shapes),
    )(*args)


def reduce_all(send):
    return lax.all_to_all(send, ("pair", "tile"), 0, 0, tiled=True)


def exchange_rows_cols(cells):
    return (
        from_prev(cells, "tile"),
        from_next(cells, "tile"),
        from_prev(cells[:, -1:], "pair"),
        from_next(cells[:, :1], "pair"),
    )


def body(phase, incidence, pair_weight):
    groups = lax.axis_size("pair")
    cols = phase.shape[2] // groups
    padded = jnp.pad(phase[:, 0, :], ((0, 0), (2, 2)))
    windows = jnp.stack([padded[:, j * cols : j * cols + cols + 4] for j in range(groups)])
    meta = jnp.stack(
        [incidence[:, 0].astype(jnp.float32), incidence[:, 1].astype(jnp.float32), pair_weight], axis=1
    )
    meta = jnp.pad(meta, ((0, 0), (0, 1)))
    chunks = jnp.concatenate([windows, jnp.broadcast_to(meta, (groups,) + meta.shape)], axis=2)
    got = lax.all_to_all(chunks, "pair", 0, 0, tiled=True).reshape(-1, chunks.shape[2])
    values = got[:, : cols + 4]
    earlier = got[:, cols + 4 : cols + 5]
    later = got[:, cols + 5 : cols + 6]
    weight = got[:, cols + 6 : cols + 7]
    dates = jnp.arange(DATES, dtype=jnp.float32)
    network = ((dates[None, :] == later).astype(jnp.float32) - (dates[None, :] == earlier).astype(jnp.float32)).astype(
        jnp.bfloat16
    )
    weighted = weight * values
    high = lax.reduce_precision(weighted, exponent_bits=8, mantissa_bits=7)
    rest = weighted - high
    middle = lax.reduce_precision(rest, exponent_bits=8, mantissa_bits=7)
    low = rest - middle
    high, middle, low = (part.astype(jnp.bfloat16) for part in (high, middle, low))
    width = values.shape[1]
    pieces = jnp.einsum(
        "kt,kc->tc", network, jnp.concatenate([high, middle, low], axis=1), preferred_element_type=jnp.float32
    )
    right_wide = pieces[:, :width] + pieces[:, width : 2 * width] + pieces[:, 2 * width :]
    span_hot = (jnp.arange(SPAN, dtype=jnp.float32)[None, :] == (later - earlier)).astype(jnp.float32)
    start_hot = (dates[None, :] == earlier).astype(jnp.float32)
    span_weights = jnp.einsum("kt,kd->td", start_hot, span_hot * weight, precision=HIGHEST)
    matrix = normal_matrix(span_weights)
    residual = right_wide[:, 2:-2]
    outer = jnp.concatenate([right_wide[:, 1], right_wide[:, -2], jnp.zeros((8 * 128 - 2 * DATES,), jnp.float32)])
    payload = jnp.concatenate([residual, outer.reshape(8, 128)], axis=0)
    above_wide = from_prev(payload, "tile")
    below_wide = from_next(payload, "tile")
    residual_halo = (above_wide, below_wide, right_wide[:, 1:2], right_wide[:, -2:-1])
    above_outer = above_wide[DATES:].reshape(-1)
    below_outer = below_wide[DATES:].reshape(-1)
    edge = jnp.stack([right_wide[:, 1], right_wide[:, -2]], axis=1)
    edge_rows = jnp.stack([above_outer[:DATES] + below_outer[:DATES], above_outer[DATES : 2 * DATES] + below_outer[DATES : 2 * DATES]], axis=1)
    edge_cols = jnp.stack([right_wide[:, 0] + right_wide[:, 2], right_wide[:, -3] + right_wide[:, -1]], axis=1)
    edge_image = jnp.dot(matrix, edge, precision=HIGHEST) - spatial_weight * (edge_rows + edge_cols)
    place = lax.axis_index("pair")
    inside = jnp.stack([place > 0, place < groups - 1]).astype(jnp.float32)
    edge_image = edge_image * inside[None, :]
    count = lax.axis_size("pair") * lax.axis_size("tile")
    field = residual.shape
    lanes = 128
    send_shape = (count, lanes)
    (w0,) = call(image_kernel, [field], matrix, residual, *residual_halo)
    w0_halo = (from_prev(w0, "tile"), from_next(w0, "tile"), edge_image[:, 0:1], edge_image[:, 1:2])
    z0, send = call(gram_kernel, [field, send_shape], matrix, residual, w0, *w0_halo)
    got = reduce_all(send)
    z0_halo = exchange_rows_cols(z0)
    r2, p1, q1, x2, w2, send, scal = call(
        block_kernel,
        [field, field, field, field, field, send_shape, (1, lanes)],
        got, matrix, residual, w0, z0, *residual_halo, *w0_halo, *z0_halo,
    )
    got = reduce_all(send)
    solution_field, residual = call(last_kernel, [field, field], got, scal, r2, p1, q1, x2, w2)
    return (solution_field[:, None, :], residual[:, None, :])


def solution(mesh):
    return jax.shard_map(
        body,
        mesh=mesh,
        in_specs=(P("pair", "tile", None), P("pair", None), P("pair")),
        out_specs=(P(None, "tile", "pair"), P(None, "tile", "pair")),
        check_vma=False,
    )
```

```python
import numpy as np
import jax
import jax.numpy as jnp
from jax import lax
from jax.sharding import PartitionSpec as P
from jax.experimental import pallas as pl
from jax.experimental.pallas import tpu as pltpu

DATES = 400
ITERS = 3
SPAN = 8

temporal_weight = 2.0
spatial_weight = 0.5
ridge_weight = 0.05

HIGHEST = lax.Precision.HIGHEST


def temporal_matrix():
    second = np.zeros((DATES - 2, DATES), np.float64)
    rows = np.arange(DATES - 2)
    second[rows, rows] = 1.0
    second[rows, rows + 1] = -2.0
    second[rows, rows + 2] = 1.0
    return (second.T @ second).astype(np.float32)


def from_prev(cells, axis):
    count = lax.axis_size(axis)
    return lax.ppermute(cells, axis, [(i, i + 1) for i in range(count - 1)])


def from_next(cells, axis):
    count = lax.axis_size(axis)
    return lax.ppermute(cells, axis, [(i + 1, i) for i in range(count - 1)])


def exchange(cells):
    return (
        from_prev(cells, "tile"),
        from_next(cells, "tile"),
        from_prev(cells[:, -1:], "pair"),
        from_next(cells[:, :1], "pair"),
    )


def neighbours(cells, halo):
    above, below, left, right = halo
    west = jnp.concatenate([left, cells[:, :-1]], axis=1)
    east = jnp.concatenate([cells[:, 1:], right], axis=1)
    return above + below + west + east


def apply_operator(matrix, cells, halo):
    return jnp.dot(matrix, cells, precision=HIGHEST) - spatial_weight * neighbours(cells, halo)


def total(parts):
    count = lax.axis_size("pair") * lax.axis_size("tile")
    sent = jnp.broadcast_to(parts[None, :], (count, parts.shape[0]))
    got = lax.all_to_all(sent, ("pair", "tile"), 0, 0, tiled=True)
    return jnp.sum(got, axis=0)


def normal_matrix(weights):
    dates = jnp.arange(DATES, dtype=jnp.int32)
    offset = dates[None, :] - dates[:, None]
    upper = jnp.zeros((DATES, DATES), jnp.float32)
    for d in range(1, SPAN):
        upper = upper + jnp.where(offset == d, -weights[:, d : d + 1], 0.0)
    coupling = upper + upper.T
    degree = -jnp.sum(coupling, axis=1)
    diagonal = degree + (4.0 * spatial_weight + ridge_weight)
    return coupling + jnp.where(offset == 0, diagonal[:, None], 0.0) + temporal_weight * temporal_matrix()


def lane_value(vector, j):
    lanes = lax.broadcasted_iota(jnp.int32, vector.shape, 1)
    return jnp.sum(jnp.where(lanes == j, vector, 0.0), axis=1, keepdims=True)


def shifted(cells, left, right):
    width = cells.shape[1]
    lanes = lax.broadcasted_iota(jnp.int32, cells.shape, 1)
    probe = pltpu.roll(lanes, 1, 1)
    forward = probe == jnp.where(lanes == 0, width - 1, lanes - 1)
    one = pltpu.roll(cells, 1, 1)
    back = pltpu.roll(cells, width - 1, 1)
    west = jnp.where(lanes == 0, left, jnp.where(forward, one, back))
    east = jnp.where(lanes == width - 1, right, jnp.where(forward, back, one))
    return west, east


def operate(matrix, cells, above, below, left, right):
    west, east = shifted(cells, left, right)
    return jnp.dot(matrix, cells, precision=HIGHEST, preferred_element_type=jnp.float32) - spatial_weight * (
        above + below + west + east
    )


def send_buffer(send_ref, values):
    lanes = lax.broadcasted_iota(jnp.int32, (1, send_ref.shape[1]), 1)
    row = jnp.zeros((1, send_ref.shape[1]), jnp.float32)
    for j, value in enumerate(values):
        row = row + jnp.where(lanes == j, jnp.sum(value, keepdims=True), 0.0)
    send_ref[...] = jnp.broadcast_to(row, send_ref.shape)


def image_kernel(k_ref, v_ref, vu_ref, vd_ref, vl_ref, vr_ref, w_out):
    w_out[...] = operate(k_ref[...], v_ref[...], vu_ref[...], vd_ref[...], vl_ref[...], vr_ref[...])


def gram_kernel(k_ref, r_ref, w_ref, wu_ref, wd_ref, wl_ref, wr_ref, z_out, send_ref):
    r = r_ref[...]
    w = w_ref[...]
    z = operate(k_ref[...], w, wu_ref[...], wd_ref[...], wl_ref[...], wr_ref[...])
    z_out[...] = z
    send_buffer(send_ref, [r * r, r * w, w * w, r * z, w * z])


def block_kernel(got_ref, k_ref, r_ref, w_ref, z_ref, ru_ref, rd_ref, rl_ref, rr_ref, wu_ref, wd_ref, wl_ref, wr_ref,
                 zu_ref, zd_ref, zl_ref, zr_ref, r_out, p_out, q_out, x_out, w_out, send_ref, scal_out):
    sums = jnp.sum(got_ref[...], axis=0, keepdims=True)
    norm_first = lane_value(sums, 0)
    curvature_first = lane_value(sums, 1)
    alpha_first = norm_first / curvature_first
    norm = norm_first - 2.0 * alpha_first * curvature_first + alpha_first * alpha_first * lane_value(sums, 2)
    beta = norm / norm_first
    a = 1.0 + beta
    b = -alpha_first
    curvature = a * a * curvature_first + a * b * (lane_value(sums, 3) + lane_value(sums, 2)) + b * b * lane_value(sums, 4)
    alpha = norm / curvature
    r0 = r_ref[...]
    w0 = w_ref[...]
    z0 = z_ref[...]
    p = a * r0 + b * w0
    q = a * w0 + b * z0
    p_out[...] = p
    q_out[...] = q
    x_out[...] = alpha_first * r0 + alpha * p
    r = (r0 - alpha_first * w0) - alpha * q
    r_out[...] = r
    halo = []
    for hr, hw, hz in zip((ru_ref, rd_ref, rl_ref, rr_ref), (wu_ref, wd_ref, wl_ref, wr_ref), (zu_ref, zd_ref, zl_ref, zr_ref)):
        halo.append((hr[...] - alpha_first * hw[...]) - alpha * (a * hw[...] + b * hz[...]))
    w = operate(k_ref[...], r, *halo)
    w_out[...] = w
    send_buffer(send_ref, [r * r, r * w, r * q, p * w, p * q])
    lanes = lax.broadcasted_iota(jnp.int32, scal_out.shape, 1)
    scal_out[...] = jnp.where(lanes == 0, norm, 0.0)


def step_scalars(got_ref, scal_ref):
    sums = jnp.sum(got_ref[...], axis=0, keepdims=True)
    previous = scal_ref[...]
    norm = lane_value(sums, 0)
    beta = norm / lane_value(previous, 0)
    curvature = lane_value(sums, 1) + beta * (lane_value(sums, 2) + lane_value(sums, 3)) + beta * beta * lane_value(sums, 4)
    return norm, beta, norm / curvature


def last_kernel(got_ref, scal_ref, r_ref, p_ref, q_ref, x_ref, w_ref, x_out, r_out):
    norm, beta, alpha = step_scalars(got_ref, scal_ref)
    p = r_ref[...] + beta * p_ref[...]
    q = w_ref[...] + beta * q_ref[...]
    x_out[...] = x_ref[...] + alpha * p
    r_out[...] = r_ref[...] - alpha * q


def call(kernel, shapes, *args):
    resident = pl.BlockSpec(memory_space=pltpu.VMEM)
    return pl.pallas_call(
        kernel,
        out_shape=[jax.ShapeDtypeStruct(s, jnp.float32) for s in shapes],
        in_specs=[resident] * len(args),
        out_specs=[resident] * len(shapes),
    )(*args)


def reduce_all(send):
    return lax.all_to_all(send, ("pair", "tile"), 0, 0, tiled=True)


def exchange_rows_cols(cells):
    return (
        from_prev(cells, "tile"),
        from_next(cells, "tile"),
        from_prev(cells[:, -1:], "pair"),
        from_next(cells[:, :1], "pair"),
    )


def body(phase, incidence, pair_weight):
    groups = lax.axis_size("pair")
    cols = phase.shape[2] // groups
    padded = jnp.pad(phase[:, 0, :], ((0, 0), (2, 2)))
    windows = jnp.stack([padded[:, j * cols : j * cols + cols + 4] for j in range(groups)])
    meta = jnp.stack(
        [incidence[:, 0].astype(jnp.float32), incidence[:, 1].astype(jnp.float32), pair_weight], axis=1
    )
    meta = jnp.pad(meta, ((0, 0), (0, 1)))
    chunks = jnp.concatenate([windows, jnp.broadcast_to(meta, (groups,) + meta.shape)], axis=2)
    got = lax.all_to_all(chunks, "pair", 0, 0, tiled=True).reshape(-1, chunks.shape[2])
    values = got[:, : cols + 4]
    earlier = got[:, cols + 4 : cols + 5]
    later = got[:, cols + 5 : cols + 6]
    weight = got[:, cols + 6 : cols + 7]
    dates = jnp.arange(DATES, dtype=jnp.float32)
    network = ((dates[None, :] == later).astype(jnp.float32) - (dates[None, :] == earlier).astype(jnp.float32)).astype(
        jnp.bfloat16
    )
    weighted = weight * values
    high = lax.reduce_precision(weighted, exponent_bits=8, mantissa_bits=7)
    rest = weighted - high
    middle = lax.reduce_precision(rest, exponent_bits=8, mantissa_bits=7)
    low = rest - middle
    high, middle, low = (part.astype(jnp.bfloat16) for part in (high, middle, low))
    width = values.shape[1]
    pieces = jnp.einsum(
        "kt,kc->tc", network, jnp.concatenate([high, middle, low], axis=1), preferred_element_type=jnp.float32
    )
    right_wide = pieces[:, :width] + pieces[:, width : 2 * width] + pieces[:, 2 * width :]
    span_hot = (jnp.arange(SPAN, dtype=jnp.float32)[None, :] == (later - earlier)).astype(jnp.float32)
    start_hot = (dates[None, :] == earlier).astype(jnp.float32)
    spread = span_hot * weight
    spread_high = lax.reduce_precision(spread, exponent_bits=8, mantissa_bits=7)
    spread_rest = spread - spread_high
    spread_middle = lax.reduce_precision(spread_rest, exponent_bits=8, mantissa_bits=7)
    spread_parts = jnp.concatenate(
        [p.astype(jnp.bfloat16) for p in (spread_high, spread_middle, spread_rest - spread_middle)], axis=1
    )
    span_pieces = jnp.einsum(
        "kt,kd->td", start_hot.astype(jnp.bfloat16), spread_parts, preferred_element_type=jnp.float32
    )
    span_weights = span_pieces[:, :SPAN] + span_pieces[:, SPAN : 2 * SPAN] + span_pieces[:, 2 * SPAN :]
    matrix = normal_matrix(span_weights)
    residual = right_wide[:, 2:-2]
    outer = jnp.concatenate([right_wide[:, 1], right_wide[:, -2], jnp.zeros((8 * 128 - 2 * DATES,), jnp.float32)])
    payload = jnp.concatenate([residual, outer.reshape(8, 128)], axis=0)
    above_wide = from_prev(payload, "tile")
    below_wide = from_next(payload, "tile")
    residual_halo = (above_wide[:DATES], below_wide[:DATES], right_wide[:, 1:2], right_wide[:, -2:-1])
    above_outer = above_wide[DATES:].reshape(-1)
    below_outer = below_wide[DATES:].reshape(-1)
    edge = jnp.stack([right_wide[:, 1], right_wide[:, -2]], axis=1)
    edge_rows = jnp.stack([above_outer[:DATES] + below_outer[:DATES], above_outer[DATES : 2 * DATES] + below_outer[DATES : 2 * DATES]], axis=1)
    edge_cols = jnp.stack([right_wide[:, 0] + right_wide[:, 2], right_wide[:, -3] + right_wide[:, -1]], axis=1)
    edge_image = jnp.dot(matrix, edge, precision=HIGHEST) - spatial_weight * (edge_rows + edge_cols)
    place = lax.axis_index("pair")
    inside = jnp.stack([place > 0, place < groups - 1]).astype(jnp.float32)
    edge_image = edge_image * inside[None, :]
    count = lax.axis_size("pair") * lax.axis_size("tile")
    field = residual.shape
    lanes = 128
    send_shape = (count, lanes)
    (w0,) = call(image_kernel, [field], matrix, residual, *residual_halo)
    w0_halo = (from_prev(w0, "tile"), from_next(w0, "tile"), edge_image[:, 0:1], edge_image[:, 1:2])
    z0, send = call(gram_kernel, [field, send_shape], matrix, residual, w0, *w0_halo)
    got = reduce_all(send)
    z0_halo = exchange_rows_cols(z0)
    r2, p1, q1, x2, w2, send, scal = call(
        block_kernel,
        [field, field, field, field, field, send_shape, (1, lanes)],
        got, matrix, residual, w0, z0, *residual_halo, *w0_halo, *z0_halo,
    )
    got = reduce_all(send)
    solution_field, residual = call(last_kernel, [field, field], got, scal, r2, p1, q1, x2, w2)
    return (solution_field[:, None, :], residual[:, None, :])


def solution(mesh):
    return jax.shard_map(
        body,
        mesh=mesh,
        in_specs=(P("pair", "tile", None), P("pair", None), P("pair")),
        out_specs=(P(None, "tile", "pair"), P(None, "tile", "pair")),
        check_vma=False,
    )
```

```python
import numpy as np
import jax
import jax.numpy as jnp
from jax import lax
from jax.sharding import PartitionSpec as P
from jax.experimental import pallas as pl
from jax.experimental.pallas import tpu as pltpu

DATES = 400
ITERS = 3
SPAN = 8

temporal_weight = 2.0
spatial_weight = 0.5
ridge_weight = 0.05

HIGHEST = lax.Precision.HIGHEST


def temporal_matrix():
    second = np.zeros((DATES - 2, DATES), np.float64)
    rows = np.arange(DATES - 2)
    second[rows, rows] = 1.0
    second[rows, rows + 1] = -2.0
    second[rows, rows + 2] = 1.0
    return (second.T @ second).astype(np.float32)


def from_prev(cells, axis):
    count = lax.axis_size(axis)
    return lax.ppermute(cells, axis, [(i, i + 1) for i in range(count - 1)])


def from_next(cells, axis):
    count = lax.axis_size(axis)
    return lax.ppermute(cells, axis, [(i + 1, i) for i in range(count - 1)])


def exchange(cells):
    return (
        from_prev(cells, "tile"),
        from_next(cells, "tile"),
        from_prev(cells[:, -1:], "pair"),
        from_next(cells[:, :1], "pair"),
    )


def neighbours(cells, halo):
    above, below, left, right = halo
    west = jnp.concatenate([left, cells[:, :-1]], axis=1)
    east = jnp.concatenate([cells[:, 1:], right], axis=1)
    return above + below + west + east


def apply_operator(matrix, cells, halo):
    return jnp.dot(matrix, cells, precision=HIGHEST) - spatial_weight * neighbours(cells, halo)


def total(parts):
    count = lax.axis_size("pair") * lax.axis_size("tile")
    sent = jnp.broadcast_to(parts[None, :], (count, parts.shape[0]))
    got = lax.all_to_all(sent, ("pair", "tile"), 0, 0, tiled=True)
    return jnp.sum(got, axis=0)


def normal_matrix(weights):
    dates = jnp.arange(DATES, dtype=jnp.int32)
    offset = dates[None, :] - dates[:, None]
    across = weights.T
    coupling = jnp.zeros((DATES, DATES), jnp.float32)
    degree = jnp.zeros((DATES,), jnp.float32)
    for d in range(1, SPAN):
        coupling = coupling + jnp.where(offset == d, -weights[:, d : d + 1], 0.0)
        coupling = coupling + jnp.where(offset == -d, -across[d : d + 1, :], 0.0)
        degree = degree + weights[:, d] + jnp.pad(weights[: DATES - d, d], (d, 0))
    diagonal = degree + (4.0 * spatial_weight + ridge_weight)
    return coupling + jnp.where(offset == 0, diagonal[:, None], 0.0) + temporal_weight * temporal_matrix()


def lane_value(vector, j):
    lanes = lax.broadcasted_iota(jnp.int32, vector.shape, 1)
    return jnp.sum(jnp.where(lanes == j, vector, 0.0), axis=1, keepdims=True)


def shifted(cells, left, right):
    width = cells.shape[1]
    lanes = lax.broadcasted_iota(jnp.int32, cells.shape, 1)
    probe = pltpu.roll(lanes, 1, 1)
    forward = probe == jnp.where(lanes == 0, width - 1, lanes - 1)
    one = pltpu.roll(cells, 1, 1)
    back = pltpu.roll(cells, width - 1, 1)
    west = jnp.where(lanes == 0, left, jnp.where(forward, one, back))
    east = jnp.where(lanes == width - 1, right, jnp.where(forward, back, one))
    return west, east


def operate(matrix, cells, above, below, left, right):
    west, east = shifted(cells, left, right)
    return jnp.dot(matrix, cells, precision=HIGHEST, preferred_element_type=jnp.float32) - spatial_weight * (
        above + below + west + east
    )


def send_buffer(send_ref, values):
    lanes = lax.broadcasted_iota(jnp.int32, (1, send_ref.shape[1]), 1)
    row = jnp.zeros((1, send_ref.shape[1]), jnp.float32)
    for j, value in enumerate(values):
        row = row + jnp.where(lanes == j, jnp.sum(value, keepdims=True), 0.0)
    send_ref[...] = jnp.broadcast_to(row, send_ref.shape)


def image_kernel(k_ref, v_ref, vu_ref, vd_ref, vl_ref, vr_ref, w_out):
    w_out[...] = operate(k_ref[...], v_ref[...], vu_ref[...], vd_ref[...], vl_ref[...], vr_ref[...])


def gram_kernel(k_ref, r_ref, w_ref, wu_ref, wd_ref, wl_ref, wr_ref, z_out, send_ref):
    r = r_ref[...]
    w = w_ref[...]
    z = operate(k_ref[...], w, wu_ref[...], wd_ref[...], wl_ref[...], wr_ref[...])
    z_out[...] = z
    send_buffer(send_ref, [r * r, r * w, w * w, r * z, w * z])


def block_kernel(got_ref, k_ref, r_ref, w_ref, z_ref, ru_ref, rd_ref, rl_ref, rr_ref, wu_ref, wd_ref, wl_ref, wr_ref,
                 zu_ref, zd_ref, zl_ref, zr_ref, r_out, p_out, q_out, x_out, w_out, send_ref, scal_out):
    sums = jnp.sum(got_ref[...], axis=0, keepdims=True)
    norm_first = lane_value(sums, 0)
    curvature_first = lane_value(sums, 1)
    alpha_first = norm_first / curvature_first
    norm = norm_first - 2.0 * alpha_first * curvature_first + alpha_first * alpha_first * lane_value(sums, 2)
    beta = norm / norm_first
    a = 1.0 + beta
    b = -alpha_first
    curvature = a * a * curvature_first + a * b * (lane_value(sums, 3) + lane_value(sums, 2)) + b * b * lane_value(sums, 4)
    alpha = norm / curvature
    r0 = r_ref[...]
    w0 = w_ref[...]
    z0 = z_ref[...]
    p = a * r0 + b * w0
    q = a * w0 + b * z0
    p_out[...] = p
    q_out[...] = q
    x_out[...] = alpha_first * r0 + alpha * p
    r = (r0 - alpha_first * w0) - alpha * q
    r_out[...] = r
    halo = []
    for hr, hw, hz in zip((ru_ref, rd_ref, rl_ref, rr_ref), (wu_ref, wd_ref, wl_ref, wr_ref), (zu_ref, zd_ref, zl_ref, zr_ref)):
        halo.append((hr[...] - alpha_first * hw[...]) - alpha * (a * hw[...] + b * hz[...]))
    w = operate(k_ref[...], r, *halo)
    w_out[...] = w
    send_buffer(send_ref, [r * r, r * w, r * q, p * w, p * q])
    lanes = lax.broadcasted_iota(jnp.int32, scal_out.shape, 1)
    scal_out[...] = jnp.where(lanes == 0, norm, 0.0)


def step_scalars(got_ref, scal_ref):
    sums = jnp.sum(got_ref[...], axis=0, keepdims=True)
    previous = scal_ref[...]
    norm = lane_value(sums, 0)
    beta = norm / lane_value(previous, 0)
    curvature = lane_value(sums, 1) + beta * (lane_value(sums, 2) + lane_value(sums, 3)) + beta * beta * lane_value(sums, 4)
    return norm, beta, norm / curvature


def last_kernel(got_ref, scal_ref, r_ref, p_ref, q_ref, x_ref, w_ref, x_out, r_out):
    norm, beta, alpha = step_scalars(got_ref, scal_ref)
    p = r_ref[...] + beta * p_ref[...]
    q = w_ref[...] + beta * q_ref[...]
    x_out[...] = x_ref[...] + alpha * p
    r_out[...] = r_ref[...] - alpha * q


def call(kernel, shapes, *args):
    resident = pl.BlockSpec(memory_space=pltpu.VMEM)
    return pl.pallas_call(
        kernel,
        out_shape=[jax.ShapeDtypeStruct(s, jnp.float32) for s in shapes],
        in_specs=[resident] * len(args),
        out_specs=[resident] * len(shapes),
    )(*args)


def reduce_all(send):
    return lax.all_to_all(send, ("pair", "tile"), 0, 0, tiled=True)


def exchange_rows_cols(cells):
    return (
        from_prev(cells, "tile"),
        from_next(cells, "tile"),
        from_prev(cells[:, -1:], "pair"),
        from_next(cells[:, :1], "pair"),
    )


def body(phase, incidence, pair_weight):
    groups = lax.axis_size("pair")
    cols = phase.shape[2] // groups
    padded = jnp.pad(phase[:, 0, :], ((0, 0), (2, 2)))
    windows = jnp.stack([padded[:, j * cols : j * cols + cols + 4] for j in range(groups)])
    meta = jnp.stack(
        [incidence[:, 0].astype(jnp.float32), incidence[:, 1].astype(jnp.float32), pair_weight], axis=1
    )
    meta = jnp.pad(meta, ((0, 0), (0, 1)))
    chunks = jnp.concatenate([windows, jnp.broadcast_to(meta, (groups,) + meta.shape)], axis=2)
    got = lax.all_to_all(chunks, "pair", 0, 0, tiled=True).reshape(-1, chunks.shape[2])
    values = got[:, : cols + 4]
    earlier = got[:, cols + 4 : cols + 5]
    later = got[:, cols + 5 : cols + 6]
    weight = got[:, cols + 6 : cols + 7]
    dates = jnp.arange(DATES, dtype=jnp.float32)
    network = ((dates[None, :] == later).astype(jnp.float32) - (dates[None, :] == earlier).astype(jnp.float32)).astype(
        jnp.bfloat16
    )
    weighted = weight * values
    high = lax.reduce_precision(weighted, exponent_bits=8, mantissa_bits=7)
    rest = weighted - high
    middle = lax.reduce_precision(rest, exponent_bits=8, mantissa_bits=7)
    low = rest - middle
    high, middle, low = (part.astype(jnp.bfloat16) for part in (high, middle, low))
    width = values.shape[1]
    pieces = jnp.einsum(
        "kt,kc->tc", network, jnp.concatenate([high, middle, low], axis=1), preferred_element_type=jnp.float32
    )
    right_wide = pieces[:, :width] + pieces[:, width : 2 * width] + pieces[:, 2 * width :]
    span_hot = (jnp.arange(SPAN, dtype=jnp.float32)[None, :] == (later - earlier)).astype(jnp.float32)
    start_hot = (dates[None, :] == earlier).astype(jnp.float32)
    spread = span_hot * weight
    spread_high = lax.reduce_precision(spread, exponent_bits=8, mantissa_bits=7)
    spread_rest = spread - spread_high
    spread_middle = lax.reduce_precision(spread_rest, exponent_bits=8, mantissa_bits=7)
    spread_parts = jnp.concatenate(
        [p.astype(jnp.bfloat16) for p in (spread_high, spread_middle, spread_rest - spread_middle)], axis=1
    )
    span_pieces = jnp.einsum(
        "kt,kd->td", start_hot.astype(jnp.bfloat16), spread_parts, preferred_element_type=jnp.float32
    )
    span_weights = span_pieces[:, :SPAN] + span_pieces[:, SPAN : 2 * SPAN] + span_pieces[:, 2 * SPAN :]
    matrix = normal_matrix(span_weights)
    residual = right_wide[:, 2:-2]
    outer = jnp.concatenate([right_wide[:, 1], right_wide[:, -2], jnp.zeros((8 * 128 - 2 * DATES,), jnp.float32)])
    payload = jnp.concatenate([residual, outer.reshape(8, 128)], axis=0)
    above_wide = from_prev(payload, "tile")
    below_wide = from_next(payload, "tile")
    residual_halo = (above_wide[:DATES], below_wide[:DATES], right_wide[:, 1:2], right_wide[:, -2:-1])
    above_outer = above_wide[DATES:].reshape(-1)
    below_outer = below_wide[DATES:].reshape(-1)
    edge = jnp.stack([right_wide[:, 1], right_wide[:, -2]], axis=1)
    edge_rows = jnp.stack([above_outer[:DATES] + below_outer[:DATES], above_outer[DATES : 2 * DATES] + below_outer[DATES : 2 * DATES]], axis=1)
    edge_cols = jnp.stack([right_wide[:, 0] + right_wide[:, 2], right_wide[:, -3] + right_wide[:, -1]], axis=1)
    edge_image = jnp.dot(matrix, edge, precision=HIGHEST) - spatial_weight * (edge_rows + edge_cols)
    place = lax.axis_index("pair")
    inside = jnp.stack([place > 0, place < groups - 1]).astype(jnp.float32)
    edge_image = edge_image * inside[None, :]
    count = lax.axis_size("pair") * lax.axis_size("tile")
    field = residual.shape
    lanes = 128
    send_shape = (count, lanes)
    (w0,) = call(image_kernel, [field], matrix, residual, *residual_halo)
    w0_halo = (from_prev(w0, "tile"), from_next(w0, "tile"), edge_image[:, 0:1], edge_image[:, 1:2])
    z0, send = call(gram_kernel, [field, send_shape], matrix, residual, w0, *w0_halo)
    got = reduce_all(send)
    z0_halo = exchange_rows_cols(z0)
    r2, p1, q1, x2, w2, send, scal = call(
        block_kernel,
        [field, field, field, field, field, send_shape, (1, lanes)],
        got, matrix, residual, w0, z0, *residual_halo, *w0_halo, *z0_halo,
    )
    got = reduce_all(send)
    solution_field, residual = call(last_kernel, [field, field], got, scal, r2, p1, q1, x2, w2)
    return (solution_field[:, None, :], residual[:, None, :])


def solution(mesh):
    return jax.shard_map(
        body,
        mesh=mesh,
        in_specs=(P("pair", "tile", None), P("pair", None), P("pair")),
        out_specs=(P(None, "tile", "pair"), P(None, "tile", "pair")),
        check_vma=False,
    )
```

```python
import numpy as np
import jax
import jax.numpy as jnp
from jax import lax
from jax.sharding import PartitionSpec as P
from jax.experimental import pallas as pl
from jax.experimental.pallas import tpu as pltpu

DATES = 400
ITERS = 3
SPAN = 8

temporal_weight = 2.0
spatial_weight = 0.5
ridge_weight = 0.05

HIGHEST = lax.Precision.HIGHEST


def temporal_matrix():
    second = np.zeros((DATES - 2, DATES), np.float64)
    rows = np.arange(DATES - 2)
    second[rows, rows] = 1.0
    second[rows, rows + 1] = -2.0
    second[rows, rows + 2] = 1.0
    return (second.T @ second).astype(np.float32)


def from_prev(cells, axis):
    count = lax.axis_size(axis)
    return lax.ppermute(cells, axis, [(i, i + 1) for i in range(count - 1)])


def from_next(cells, axis):
    count = lax.axis_size(axis)
    return lax.ppermute(cells, axis, [(i + 1, i) for i in range(count - 1)])


def exchange(cells):
    return (
        from_prev(cells, "tile"),
        from_next(cells, "tile"),
        from_prev(cells[:, -1:], "pair"),
        from_next(cells[:, :1], "pair"),
    )


def neighbours(cells, halo):
    above, below, left, right = halo
    west = jnp.concatenate([left, cells[:, :-1]], axis=1)
    east = jnp.concatenate([cells[:, 1:], right], axis=1)
    return above + below + west + east


def apply_operator(matrix, cells, halo):
    return jnp.dot(matrix, cells, precision=HIGHEST) - spatial_weight * neighbours(cells, halo)


def total(parts):
    count = lax.axis_size("pair") * lax.axis_size("tile")
    sent = jnp.broadcast_to(parts[None, :], (count, parts.shape[0]))
    got = lax.all_to_all(sent, ("pair", "tile"), 0, 0, tiled=True)
    return jnp.sum(got, axis=0)


def normal_matrix(weights):
    dates = jnp.arange(DATES, dtype=jnp.int32)
    offset = dates[None, :] - dates[:, None]
    upper = jnp.zeros((DATES, DATES), jnp.float32)
    for d in range(1, SPAN):
        upper = upper + jnp.where(offset == d, -weights[:, d : d + 1], 0.0)
    coupling = upper + upper.T
    degree = -jnp.sum(coupling, axis=1)
    diagonal = degree + (4.0 * spatial_weight + ridge_weight)
    return coupling + jnp.where(offset == 0, diagonal[:, None], 0.0) + temporal_weight * temporal_matrix()


def lane_value(vector, j):
    lanes = lax.broadcasted_iota(jnp.int32, vector.shape, 1)
    return jnp.sum(jnp.where(lanes == j, vector, 0.0), axis=1, keepdims=True)


def shifted(cells, left, right):
    width = cells.shape[1]
    lanes = lax.broadcasted_iota(jnp.int32, cells.shape, 1)
    probe = pltpu.roll(lanes, 1, 1)
    forward = probe == jnp.where(lanes == 0, width - 1, lanes - 1)
    one = pltpu.roll(cells, 1, 1)
    back = pltpu.roll(cells, width - 1, 1)
    west = jnp.where(lanes == 0, left, jnp.where(forward, one, back))
    east = jnp.where(lanes == width - 1, right, jnp.where(forward, back, one))
    return west, east


def operate(matrix, cells, above, below, left, right):
    west, east = shifted(cells, left, right)
    return jnp.dot(matrix, cells, precision=HIGHEST, preferred_element_type=jnp.float32) - spatial_weight * (
        above + below + west + east
    )


def send_buffer(send_ref, values):
    lanes = lax.broadcasted_iota(jnp.int32, (1, send_ref.shape[1]), 1)
    row = jnp.zeros((1, send_ref.shape[1]), jnp.float32)
    for j, value in enumerate(values):
        row = row + jnp.where(lanes == j, jnp.sum(value, keepdims=True), 0.0)
    send_ref[...] = jnp.broadcast_to(row, send_ref.shape)


def image_kernel(k_ref, v_ref, vu_ref, vd_ref, vl_ref, vr_ref, w_out):
    w_out[...] = operate(k_ref[...], v_ref[...], vu_ref[...], vd_ref[...], vl_ref[...], vr_ref[...])


def gram_kernel(k_ref, r_ref, w_ref, wu_ref, wd_ref, wl_ref, wr_ref, z_out, send_ref):
    r = r_ref[...]
    w = w_ref[...]
    z = operate(k_ref[...], w, wu_ref[...], wd_ref[...], wl_ref[...], wr_ref[...])
    z_out[...] = z
    send_buffer(send_ref, [r * r, r * w, w * w, r * z, w * z])


def block_kernel(got_ref, k_ref, r_ref, w_ref, z_ref, ru_ref, rd_ref, rl_ref, rr_ref, wu_ref, wd_ref, wl_ref, wr_ref,
                 zu_ref, zd_ref, zl_ref, zr_ref, r_out, p_out, q_out, x_out, w_out, send_ref, scal_out):
    sums = jnp.sum(got_ref[...], axis=0, keepdims=True)
    norm_first = lane_value(sums, 0)
    curvature_first = lane_value(sums, 1)
    alpha_first = norm_first / curvature_first
    norm = norm_first - 2.0 * alpha_first * curvature_first + alpha_first * alpha_first * lane_value(sums, 2)
    beta = norm / norm_first
    a = 1.0 + beta
    b = -alpha_first
    curvature = a * a * curvature_first + a * b * (lane_value(sums, 3) + lane_value(sums, 2)) + b * b * lane_value(sums, 4)
    alpha = norm / curvature
    r0 = r_ref[...]
    w0 = w_ref[...]
    z0 = z_ref[...]
    p = a * r0 + b * w0
    q = a * w0 + b * z0
    p_out[...] = p
    q_out[...] = q
    x_out[...] = alpha_first * r0 + alpha * p
    r = (r0 - alpha_first * w0) - alpha * q
    r_out[...] = r
    halo = []
    for hr, hw, hz in zip((ru_ref, rd_ref, rl_ref, rr_ref), (wu_ref, wd_ref, wl_ref, wr_ref), (zu_ref, zd_ref, zl_ref, zr_ref)):
        halo.append((hr[...] - alpha_first * hw[...]) - alpha * (a * hw[...] + b * hz[...]))
    w = operate(k_ref[...], r, *halo)
    w_out[...] = w
    send_buffer(send_ref, [r * r, r * w, r * q, p * w, p * q])
    lanes = lax.broadcasted_iota(jnp.int32, scal_out.shape, 1)
    scal_out[...] = jnp.where(lanes == 0, norm, 0.0)


def step_scalars(got_ref, scal_ref):
    sums = jnp.sum(got_ref[...], axis=0, keepdims=True)
    previous = scal_ref[...]
    norm = lane_value(sums, 0)
    beta = norm / lane_value(previous, 0)
    curvature = lane_value(sums, 1) + beta * (lane_value(sums, 2) + lane_value(sums, 3)) + beta * beta * lane_value(sums, 4)
    return norm, beta, norm / curvature


def last_kernel(got_ref, scal_ref, r_ref, p_ref, q_ref, x_ref, w_ref, x_out, r_out):
    norm, beta, alpha = step_scalars(got_ref, scal_ref)
    p = r_ref[...] + beta * p_ref[...]
    q = w_ref[...] + beta * q_ref[...]
    x_out[...] = x_ref[...] + alpha * p
    r_out[...] = r_ref[...] - alpha * q


def call(kernel, shapes, *args):
    resident = pl.BlockSpec(memory_space=pltpu.VMEM)
    return pl.pallas_call(
        kernel,
        out_shape=[jax.ShapeDtypeStruct(s, jnp.float32) for s in shapes],
        in_specs=[resident] * len(args),
        out_specs=[resident] * len(shapes),
    )(*args)


def reduce_all(send):
    return lax.all_to_all(send, ("pair", "tile"), 0, 0, tiled=True)


def exchange_rows_cols(cells):
    return (
        from_prev(cells, "tile"),
        from_next(cells, "tile"),
        from_prev(cells[:, -1:], "pair"),
        from_next(cells[:, :1], "pair"),
    )


def body(phase, incidence, pair_weight):
    groups = lax.axis_size("pair")
    cols = phase.shape[2] // groups
    padded = jnp.pad(phase[:, 0, :], ((0, 0), (2, 2)))
    width = groups * cols
    blocks = padded[:, 2 : width + 2].reshape(-1, groups, cols)
    below_block = padded[:, :width].reshape(-1, groups, cols)[:, :, :2]
    above_block = padded[:, 4 : width + 4].reshape(-1, groups, cols)[:, :, cols - 2 :]
    windows = jnp.concatenate([below_block, blocks, above_block], axis=2)
    meta = jnp.stack(
        [incidence[:, 0].astype(jnp.float32), incidence[:, 1].astype(jnp.float32), pair_weight], axis=1
    )
    meta = jnp.pad(meta, ((0, 0), (0, 1)))
    chunks = jnp.concatenate([windows, jnp.broadcast_to(meta[:, None, :], (meta.shape[0], groups, meta.shape[1]))], axis=2)
    got = lax.all_to_all(chunks, "pair", 1, 0, tiled=True).reshape(-1, chunks.shape[2])
    values = got[:, : cols + 4]
    earlier = got[:, cols + 4 : cols + 5]
    later = got[:, cols + 5 : cols + 6]
    weight = got[:, cols + 6 : cols + 7]
    dates = jnp.arange(DATES, dtype=jnp.float32)
    network = ((dates[None, :] == later).astype(jnp.float32) - (dates[None, :] == earlier).astype(jnp.float32)).astype(
        jnp.bfloat16
    )
    weighted = weight * values
    high = lax.reduce_precision(weighted, exponent_bits=8, mantissa_bits=7)
    rest = weighted - high
    middle = lax.reduce_precision(rest, exponent_bits=8, mantissa_bits=7)
    low = rest - middle
    high, middle, low = (part.astype(jnp.bfloat16) for part in (high, middle, low))
    width = values.shape[1]
    pieces = jnp.einsum(
        "kt,kc->tc", network, jnp.concatenate([high, middle, low], axis=1), preferred_element_type=jnp.float32
    )
    right_wide = pieces[:, :width] + pieces[:, width : 2 * width] + pieces[:, 2 * width :]
    span_hot = (jnp.arange(SPAN, dtype=jnp.float32)[None, :] == (later - earlier)).astype(jnp.float32)
    start_hot = (dates[None, :] == earlier).astype(jnp.float32)
    spread = span_hot * weight
    spread_high = lax.reduce_precision(spread, exponent_bits=8, mantissa_bits=7)
    spread_rest = spread - spread_high
    spread_middle = lax.reduce_precision(spread_rest, exponent_bits=8, mantissa_bits=7)
    spread_parts = jnp.concatenate(
        [p.astype(jnp.bfloat16) for p in (spread_high, spread_middle, spread_rest - spread_middle)], axis=1
    )
    span_pieces = jnp.einsum(
        "kt,kd->td", start_hot.astype(jnp.bfloat16), spread_parts, preferred_element_type=jnp.float32
    )
    span_weights = span_pieces[:, :SPAN] + span_pieces[:, SPAN : 2 * SPAN] + span_pieces[:, 2 * SPAN :]
    matrix = normal_matrix(span_weights)
    residual = right_wide[:, 2:-2]
    outer = jnp.concatenate([right_wide[:, 1], right_wide[:, -2], jnp.zeros((8 * 128 - 2 * DATES,), jnp.float32)])
    payload = jnp.concatenate([residual, outer.reshape(8, 128)], axis=0)
    above_wide = from_prev(payload, "tile")
    below_wide = from_next(payload, "tile")
    residual_halo = (above_wide[:DATES], below_wide[:DATES], right_wide[:, 1:2], right_wide[:, -2:-1])
    above_outer = above_wide[DATES:].reshape(-1)
    below_outer = below_wide[DATES:].reshape(-1)
    edge = jnp.stack([right_wide[:, 1], right_wide[:, -2]], axis=1)
    edge_rows = jnp.stack([above_outer[:DATES] + below_outer[:DATES], above_outer[DATES : 2 * DATES] + below_outer[DATES : 2 * DATES]], axis=1)
    edge_cols = jnp.stack([right_wide[:, 0] + right_wide[:, 2], right_wide[:, -3] + right_wide[:, -1]], axis=1)
    edge_image = jnp.dot(matrix, edge, precision=HIGHEST) - spatial_weight * (edge_rows + edge_cols)
    place = lax.axis_index("pair")
    inside = jnp.stack([place > 0, place < groups - 1]).astype(jnp.float32)
    edge_image = edge_image * inside[None, :]
    count = lax.axis_size("pair") * lax.axis_size("tile")
    field = residual.shape
    lanes = 128
    send_shape = (count, lanes)
    (w0,) = call(image_kernel, [field], matrix, residual, *residual_halo)
    w0_halo = (from_prev(w0, "tile"), from_next(w0, "tile"), edge_image[:, 0:1], edge_image[:, 1:2])
    z0, send = call(gram_kernel, [field, send_shape], matrix, residual, w0, *w0_halo)
    got = reduce_all(send)
    z0_halo = exchange_rows_cols(z0)
    r2, p1, q1, x2, w2, send, scal = call(
        block_kernel,
        [field, field, field, field, field, send_shape, (1, lanes)],
        got, matrix, residual, w0, z0, *residual_halo, *w0_halo, *z0_halo,
    )
    got = reduce_all(send)
    solution_field, residual = call(last_kernel, [field, field], got, scal, r2, p1, q1, x2, w2)
    return (solution_field[:, None, :], residual[:, None, :])


def solution(mesh):
    return jax.shard_map(
        body,
        mesh=mesh,
        in_specs=(P("pair", "tile", None), P("pair", None), P("pair")),
        out_specs=(P(None, "tile", "pair"), P(None, "tile", "pair")),
        check_vma=False,
    )
```
